256 devices in a mesh: seq: 32 (over x_hi, z, core), tensor: 8 (over y, x_lo).
Axes of the slice: x: 4 (x_hi: 2, x_lo: 2; x = x_hi * 2 + x_lo), y: 4, z: 8, core: 2. Of those that a mesh axis runs over, the one named last changes fastest.
Arguments:
- tokens: bfloat16 [4, 1024, 4096], P(None, 'seq', 'tensor'), may hold values from -600 to 600
- norm_gain: bfloat16 [4096], replicated, may hold values from 0.099609375 to 1.8984375
- w_query: bfloat16 [4096, 2048], P(None, 'tensor'), may hold values from -0.1875 to 0.1875
- w_key: bfloat16 [4096, 2048], P(None, 'tensor'), may hold values from -0.09375 to 0.09375
- w_value: bfloat16 [4096, 2048], P(None, 'tensor'), may hold values from -0.09375 to 0.09375
- w_out: bfloat16 [2048, 4096], P('tensor'), may hold values from -1 to 1
- cache_keys: bfloat16 [4, 8192, 2048], P(None, 'seq', 'tensor'), may hold values from -103 to 103
- cache_values: bfloat16 [4, 8192, 2048], P(None, 'seq', 'tensor'), may hold values from -6 to 6
- cache_len: int32 [4], replicated, may hold values from 1 to 8192, as said below
- group_len: int32 [4], replicated, may hold values from 1 to 1024, 3584 in all
Outputs:
- mixed: bfloat16 [4, 1024, 4096], P(None, 'seq', 'tensor')
- new_keys: bfloat16 [4, 1024, 2048], P(None, 'seq', 'tensor')
- new_values: bfloat16 [4, 1024, 2048], P(None, 'seq', 'tensor')
The draws below stay inside these ranges and needn't reach their ends.
Inputs may be any that keep to these rules, and one draw needn't show every extreme that they name: `cache_len`: one request's cache holds all 8192 positions. `group_len`: the new-token counts sum to 3584.
All inputs are finite; a program needn't handle non-finite values.
Results may differ from the reference program's by a relative error of at most 0.0075.
The reference program's roundings to bfloat16 on the way (of `normed`, `queries`, `fresh_keys`, `fresh_values` and `attended`) count: a program that leaves them out, or rounds other values in their place, can miss the bound.
Values may be sent and summed in bfloat16 or wider, within the bound.
No kernel may reach another device: no remote copies, remote signals or barrier semaphores. Data moves between devices by JAX's collectives and lax.ppermute only.
A program may use at most 128 MiB of HBM per device.

```python
import math
from functools import partial
import jax
import jax.numpy as jnp
import numpy as np
from jax import lax

D = 4096
HD = 128
HEADS = 16
REQ = 4
CH_DEV = 32
CACHE_DEV = 256
GROUP = 1024
CAP = 8192
N_SEQ = 32


def draw_tokens(key, part):
    base_key, row_key = jax.random.split(key, 2)
    column_scale = 10.0 ** (jnp.arange(D, dtype=jnp.float32) / D)
    base = jnp.clip(jax.random.normal(base_key, (REQ, GROUP, D), jnp.float32), -6.0, 6.0)
    row_scale = 10.0 ** jax.random.uniform(row_key, (REQ, GROUP, 1), jnp.float32, 0.0, 1.0)
    return (base * column_scale * row_scale).astype(jnp.bfloat16)


def draw_cache_keys(key, part):
    base_key = jax.random.fold_in(key, 0)
    values = jnp.clip(jax.random.normal(base_key, (REQ, CAP, HEADS * HD), jnp.float32), -6.0, 6.0)
    return values.astype(jnp.bfloat16)


def draw_cache_len(key, part):
    short_key, long_key = jax.random.split(jax.random.fold_in(key, 7), 2)
    shorter = jax.random.randint(short_key, (REQ,), 1, CAP // 4 + 1)
    longest = jax.random.randint(long_key, (), 0, REQ)
    return jnp.where(jnp.arange(REQ) == longest, CAP, shorter).astype(jnp.int32)


def level_of(key, dims, pieces, smallest, largest):
    def one(axis_at, blocks):
        steps = jax.random.uniform(jax.random.fold_in(jax.random.fold_in(key, 6), axis_at), (blocks,), jnp.float32, smallest / len(pieces), largest / len(pieces))
        return jnp.repeat(jnp.exp(steps), dims[axis_at] // blocks).reshape((-1,) + (1,) * (len(dims) - axis_at - 1))

    factor_of = one(*pieces[0])
    for cut in pieces[1:]:
        factor_of = factor_of * one(*cut)
    return factor_of


def length_profile(count, total, bound, skew):
    loads = [(1 << 20) // math.isqrt(grade ** skew) + 1 for grade in range(2, count + 1)]
    surplus, holding = total - bound - (count - 1), [1] * (count - 1)
    while surplus > 0:
        movable = [i for i in range(count - 1) if holding[i] < bound]
        pool, left = sum([loads[i] for i in movable]), surplus
        for i in movable:
            addition = min(bound - holding[i], max(1, left * loads[i] // pool), surplus)
            holding[i] = holding[i] + addition
            surplus = surplus - addition
    return np.array([bound] + holding)


def ragged(stream_key, count, total, bound, lean):
    if count == 2:
        one = jax.random.randint(stream_key, (), max(1, total - bound), min(bound, total - 1) + 1)
        return jnp.stack([one, total - one])
    tallies = jnp.asarray(length_profile(count, total, bound, lean), jnp.int32)
    couples = (count - 1) // 2
    source_of, taker = tallies[1:1 + 2 * couples:2], tallies[2:2 + 2 * couples:2]
    margin = jnp.minimum(source_of - 1, bound - taker)
    passed = jax.random.randint(jax.random.fold_in(stream_key, 1), (couples,), 0, 1 << 20) % (margin + 1)
    tallies = tallies.at[1:1 + 2 * couples:2].set(source_of - passed).at[2:2 + 2 * couples:2].set(taker + passed)
    return tallies[jax.random.permutation(jax.random.fold_in(stream_key, 2), count)]


def centred(stream_key, dims, scale, most, pieces=(), held_as=jnp.bfloat16):
    drawn = scale * jax.random.normal(stream_key, dims, jnp.float32)
    if pieces:
        drawn = drawn * level_of(stream_key, dims, pieces, -0.22, 0.18)
    return jnp.clip(drawn, -most, most).astype(held_as)


def setup_inputs(seed: int = 0) -> dict:
    splits = jax.random.split(jax.random.key(seed), 11)
    return {
        "tokens": draw_tokens(jax.random.fold_in(splits[10], 71), 0),
        "norm_gain": jnp.clip(1.0 + 0.18 * jax.random.normal(splits[1], (D,), jnp.float32), 0.099609375, 1.8984375).astype(jnp.bfloat16),
        "w_query": centred(splits[2], (D, HEADS * HD), (D // 4) ** -0.5, 0.1875, ((1, 8),)),
        "w_key": centred(splits[3], (D, HEADS * HD), D ** -0.5, 0.09375, ((1, 8),)),
        "w_value": centred(splits[4], (D, HEADS * HD), D ** -0.5, 0.09375, ((1, 8),)),
        "w_out": centred(splits[5], (HEADS * HD, D), (HD // 4) ** -0.5, 1.0, ((0, 8),)),
        "cache_keys": draw_cache_keys(jax.random.fold_in(splits[10], 71), 0),
        "cache_values": centred(splits[7], (REQ, CAP, HEADS * HD), 1.0, 6.0, ((1, 32), (2, 8))),
        "cache_len": draw_cache_len(jax.random.fold_in(splits[10], 71), 0),
        "group_len": ragged(splits[9], REQ, 7 * GROUP // 2, GROUP, 0).astype(jnp.int32),
    }


def rotate(vector, position):
    half_dim = vector.shape[-1] // 2
    frequency = 1000000.0 ** (-(jnp.arange(half_dim, dtype=jnp.float32) * 2.0 / vector.shape[-1]))
    angles = position.astype(jnp.float32)[..., None] * frequency
    cosine = jnp.concatenate([jnp.cos(angles), jnp.cos(angles)], -1)[..., None, :]
    sine = jnp.concatenate([jnp.sin(angles), jnp.sin(angles)], -1)[..., None, :]
    turned = jnp.concatenate([-vector[..., half_dim:], vector[..., :half_dim]], -1)
    return vector * cosine + turned * sine

def head_attention(operands, cache_length, group_length):
    head_queries, cache_k, cache_v, group_k, group_v = operands
    key_rows = jnp.concatenate([cache_k.reshape(N_SEQ, CACHE_DEV, HD), group_k.reshape(N_SEQ, CH_DEV, HD)], 1).astype(jnp.float32)
    value_rows = jnp.concatenate([cache_v.reshape(N_SEQ, CACHE_DEV, HD), group_v.reshape(N_SEQ, CH_DEV, HD)], 1).astype(jnp.float32)
    scores = jnp.einsum('qd,nkd->qnk', head_queries.astype(jnp.float32), key_rows) * HD ** (-0.5)
    slot_index = (jnp.arange(N_SEQ)[:, None] * CACHE_DEV + jnp.arange(CACHE_DEV)[None, :]).astype(jnp.int32)
    cache_ok = slot_index < cache_length
    group_index = (jnp.arange(N_SEQ)[:, None] * CH_DEV + jnp.arange(CH_DEV)[None, :]).astype(jnp.int32)
    query_index = jnp.arange(GROUP).astype(jnp.int32)
    group_ok = (group_index[None] <= query_index[:, None, None]) & (group_index < group_length)[None]
    usable = jnp.concatenate([jnp.broadcast_to(cache_ok[None], (GROUP, N_SEQ, CACHE_DEV)), group_ok], -1)
    row_peak = lax.optimization_barrier(jnp.max(jnp.where(usable, scores, -1e+30), -1))
    weights = jnp.where(usable, jnp.exp(scores - row_peak[..., None]), 0.0)
    row_mass = lax.optimization_barrier(jnp.sum(weights, -1))
    rounded = lax.optimization_barrier(weights.astype(jnp.bfloat16))
    numerators = jnp.einsum('qnk,nkd->qnd', rounded.astype(jnp.float32), value_rows)
    top_peak = lax.optimization_barrier(jnp.max(row_peak, -1))
    factor = jnp.exp(row_peak - top_peak[:, None])
    return lax.optimization_barrier(jnp.sum(numerators * factor[..., None], 1)) / lax.optimization_barrier(jnp.sum(row_mass * factor, -1))[:, None]

def reference(tokens, norm_gain, w_query, w_key, w_value, w_out, cache_keys, cache_values, cache_len, group_len):
    widened = tokens.astype(jnp.float32)
    inverse_rms = lax.rsqrt(lax.optimization_barrier(jnp.mean(widened * widened, -1, keepdims=True)) + 1e-05)
    normed = (widened * inverse_rms * norm_gain.astype(jnp.float32)).astype(jnp.bfloat16)
    flat_rows = normed.reshape(REQ * GROUP, D)

    def project(weight):
        return jnp.dot(flat_rows, weight, preferred_element_type=jnp.float32).reshape(REQ, GROUP, HEADS, HD)
    offsets = jnp.arange(GROUP).astype(jnp.int32)
    position = cache_len[:, None] + offsets[None, :]
    queries = lax.optimization_barrier(rotate(project(w_query), position).astype(jnp.bfloat16))
    fresh_keys = lax.optimization_barrier(rotate(project(w_key), position).astype(jnp.bfloat16))
    fresh_values = lax.optimization_barrier(project(w_value).astype(jnp.bfloat16))
    live_rows = offsets[None, :] < group_len[:, None]
    collected = []
    for request in range(REQ):
        operands = (jnp.transpose(queries[request], (1, 0, 2)), jnp.transpose(cache_keys[request].reshape(CAP, HEADS, HD), (1, 0, 2)), jnp.transpose(cache_values[request].reshape(CAP, HEADS, HD), (1, 0, 2)), jnp.transpose(fresh_keys[request], (1, 0, 2)), jnp.transpose(fresh_values[request], (1, 0, 2)))
        per_head = lax.map(partial(head_attention, cache_length=cache_len[request], group_length=group_len[request]), operands)
        collected.append(jnp.transpose(per_head, (1, 0, 2)))
    attended = jnp.stack(collected)
    attended = jnp.where(live_rows[..., None, None], attended, 0.0).astype(jnp.bfloat16).reshape(REQ * GROUP, HEADS * HD)
    mixed = jnp.dot(attended, w_out, preferred_element_type=jnp.float32).astype(jnp.bfloat16).reshape(REQ, GROUP, D)
    key_flat = fresh_keys.reshape(REQ, GROUP, HEADS * HD)
    value_flat = fresh_values.reshape(REQ, GROUP, HEADS * HD)
    new_keys = jnp.where(live_rows[..., None], key_flat, jnp.zeros_like(key_flat))
    new_values = jnp.where(live_rows[..., None], value_flat, jnp.zeros_like(value_flat))
    return (mixed, new_keys, new_values)
```

```python
import jax
import jax.numpy as jnp
from jax import lax
from jax.sharding import PartitionSpec as P

HD = 128


def rotate(vector, position):
    half_dim = vector.shape[-1] // 2
    frequency = 1000000.0 ** (-(jnp.arange(half_dim, dtype=jnp.float32) * 2.0 / vector.shape[-1]))
    angles = position.astype(jnp.float32)[..., None] * frequency
    cosine = jnp.concatenate([jnp.cos(angles), jnp.cos(angles)], -1)[..., None, :]
    sine = jnp.concatenate([jnp.sin(angles), jnp.sin(angles)], -1)[..., None, :]
    turned = jnp.concatenate([-vector[..., half_dim:], vector[..., :half_dim]], -1)
    return vector * cosine + turned * sine


def body(
    tokens,
    norm_gain,
    w_query,
    w_key,
    w_value,
    w_out,
    cache_keys,
    cache_values,
    cache_len,
    group_len,
):
    seq_index = lax.axis_index("seq")
    requests, local_rows, width_part = tokens.shape
    gathered = lax.all_gather(tokens, "tensor", axis=2, tiled=True).astype(jnp.float32)
    inverse_rms = lax.rsqrt(jnp.mean(gathered * gathered, -1, keepdims=True) + 1e-05)
    normed = (gathered * inverse_rms * norm_gain.astype(jnp.float32)).astype(jnp.bfloat16)
    flat_rows = normed.reshape(requests * local_rows, -1)
    heads_width = w_query.shape[1]
    local_heads = heads_width // HD

    def project(weight):
        return jnp.dot(flat_rows, weight, preferred_element_type=jnp.float32).reshape(
            requests, local_rows, local_heads, HD
        )

    offsets = jnp.arange(local_rows, dtype=jnp.int32)
    first_row = seq_index * local_rows
    position = cache_len[:, None] + first_row + offsets[None, :]
    queries = (
        rotate(project(w_query), position)
        .astype(jnp.bfloat16)
        .reshape(requests, local_rows, heads_width)
    )
    key_new = (
        rotate(project(w_key), position)
        .astype(jnp.bfloat16)
        .reshape(requests, local_rows, heads_width)
    )
    value_new = project(w_value).astype(jnp.bfloat16).reshape(requests, local_rows, heads_width)
    live_rows = (first_row + offsets)[None, :] < group_len[:, None]
    new_keys = jnp.where(live_rows[..., None], key_new, jnp.zeros_like(key_new))
    new_values = jnp.where(live_rows[..., None], value_new, jnp.zeros_like(value_new))
    all_queries = lax.all_gather(queries, "seq", axis=1, tiled=True)
    group_total = all_queries.shape[1]
    cache_slots = cache_keys.shape[1]
    block_keys = cache_slots + local_rows
    slot_index = seq_index * cache_slots + jnp.arange(cache_slots, dtype=jnp.int32)
    query_index = jnp.arange(group_total, dtype=jnp.int32)
    token_index = first_row + offsets
    score_scale = HD ** (-0.5)
    numer_list = []
    peak_list = []
    mass_list = []
    for request in range(requests):
        query_rows = all_queries[request].reshape(group_total, local_heads, HD)
        key_rows = jnp.concatenate([cache_keys[request], key_new[request]], 0).reshape(
            block_keys, local_heads, HD
        )
        value_rows = jnp.concatenate([cache_values[request], value_new[request]], 0).reshape(
            block_keys, local_heads, HD
        )
        scores = (
            jnp.einsum("qhd,khd->hqk", query_rows, key_rows, preferred_element_type=jnp.float32)
            * score_scale
        )
        cache_ok = slot_index < cache_len[request]
        group_ok = (token_index[None, :] <= query_index[:, None]) & (
            token_index < group_len[request]
        )[None, :]
        usable = jnp.concatenate(
            [jnp.broadcast_to(cache_ok[None, :], (group_total, cache_slots)), group_ok], 1
        )[None]
        row_peak = jnp.max(jnp.where(usable, scores, -1e30), -1)
        weights = jnp.where(usable, jnp.exp(scores - row_peak[..., None]), 0.0)
        row_mass = jnp.sum(weights, -1)
        numer_list.append(
            jnp.einsum(
                "hqk,khd->qhd",
                weights.astype(jnp.bfloat16),
                value_rows,
                preferred_element_type=jnp.float32,
            )
        )
        peak_list.append(row_peak.T)
        mass_list.append(row_mass.T)
    numerators = jnp.stack(numer_list)
    row_peaks = jnp.stack(peak_list)
    row_masses = jnp.stack(mass_list)
    seq_count = group_total // local_rows
    all_peaks = lax.all_gather(row_peaks.astype(jnp.bfloat16), "seq", axis=0)
    top_peak = jnp.max(all_peaks, 0).astype(row_peaks.dtype)
    factor = jnp.exp(row_peaks - top_peak)
    scaled = (numerators * factor[..., None]).reshape(requests, group_total, heads_width)
    numer_sum, mass_sum = (
        lax.psum_scatter(scaled, "seq", scatter_dimension=1, tiled=True),
        lax.psum_scatter(row_masses * factor, "seq", scatter_dimension=1, tiled=True),
    )
    attended = numer_sum.reshape(requests, local_rows, local_heads, HD) / mass_sum[..., None]
    attended = (
        jnp.where(live_rows[..., None, None], attended, 0.0)
        .astype(jnp.bfloat16)
        .reshape(requests * local_rows, heads_width)
    )
    partial_out = jnp.dot(attended, w_out, preferred_element_type=jnp.float32).reshape(
        requests, local_rows, -1
    )
    mixed = lax.psum_scatter(partial_out, "tensor", scatter_dimension=2, tiled=True).astype(
        jnp.bfloat16
    )
    return (mixed, new_keys, new_values)


def solution(mesh):
    placed = (
        P(None, "seq", "tensor"),
        P(),
        P(None, "tensor"),
        P(None, "tensor"),
        P(None, "tensor"),
        P("tensor", None),
        P(None, "seq", "tensor"),
        P(None, "seq", "tensor"),
        P(),
        P(),
    )
    return jax.shard_map(
        body,
        mesh=mesh,
        in_specs=placed,
        out_specs=(P(None, "seq", "tensor"), P(None, "seq", "tensor"), P(None, "seq", "tensor")),
        check_vma=False,
    )
```

```python
import jax
import jax.numpy as jnp
from jax import lax
from jax.sharding import PartitionSpec as P

HD = 128


def rotate(vector, position):
    half_dim = vector.shape[-1] // 2
    frequency = 1000000.0 ** (-(jnp.arange(half_dim, dtype=jnp.float32) * 2.0 / vector.shape[-1]))
    angles = position.astype(jnp.float32)[..., None] * frequency
    cosine = jnp.concatenate([jnp.cos(angles), jnp.cos(angles)], -1)[..., None, :]
    sine = jnp.concatenate([jnp.sin(angles), jnp.sin(angles)], -1)[..., None, :]
    turned = jnp.concatenate([-vector[..., half_dim:], vector[..., :half_dim]], -1)
    return vector * cosine + turned * sine


def body(
    tokens,
    norm_gain,
    w_query,
    w_key,
    w_value,
    w_out,
    cache_keys,
    cache_values,
    cache_len,
    group_len,
):
    seq_index = lax.axis_index("seq")
    requests, local_rows, width_part = tokens.shape
    gathered = lax.all_gather(tokens, "tensor", axis=2, tiled=True).astype(jnp.float32)
    inverse_rms = lax.rsqrt(jnp.mean(gathered * gathered, -1, keepdims=True) + 1e-05)
    normed = (gathered * inverse_rms * norm_gain.astype(jnp.float32)).astype(jnp.bfloat16)
    flat_rows = normed.reshape(requests * local_rows, -1)
    heads_width = w_query.shape[1]
    local_heads = heads_width // HD

    def project(weight):
        return jnp.dot(flat_rows, weight, preferred_element_type=jnp.float32).reshape(
            requests, local_rows, local_heads, HD
        )

    offsets = jnp.arange(local_rows, dtype=jnp.int32)
    first_row = seq_index * local_rows
    position = cache_len[:, None] + first_row + offsets[None, :]
    queries = (
        rotate(project(w_query), position)
        .astype(jnp.bfloat16)
        .reshape(requests, local_rows, heads_width)
    )
    key_new = (
        rotate(project(w_key), position)
        .astype(jnp.bfloat16)
        .reshape(requests, local_rows, heads_width)
    )
    value_new = project(w_value).astype(jnp.bfloat16).reshape(requests, local_rows, heads_width)
    live_rows = (first_row + offsets)[None, :] < group_len[:, None]
    new_keys = jnp.where(live_rows[..., None], key_new, jnp.zeros_like(key_new))
    new_values = jnp.where(live_rows[..., None], value_new, jnp.zeros_like(value_new))
    all_queries = lax.all_gather(queries, "seq", axis=1, tiled=True)
    group_total = all_queries.shape[1]
    cache_slots = cache_keys.shape[1]
    block_keys = cache_slots + local_rows
    slot_index = seq_index * cache_slots + jnp.arange(cache_slots, dtype=jnp.int32)
    query_index = jnp.arange(group_total, dtype=jnp.int32)
    token_index = first_row + offsets
    score_scale = HD ** (-0.5)
    numer_list = []
    peak_list = []
    mass_list = []
    for request in range(requests):
        query_rows = all_queries[request].reshape(group_total, local_heads, HD)
        key_rows = jnp.concatenate([cache_keys[request], key_new[request]], 0).reshape(
            block_keys, local_heads, HD
        )
        value_rows = jnp.concatenate([cache_values[request], value_new[request]], 0).reshape(
            block_keys, local_heads, HD
        )
        scores = (
            jnp.einsum("qhd,khd->hqk", query_rows, key_rows, preferred_element_type=jnp.float32)
            * score_scale
        )
        cache_ok = slot_index < cache_len[request]
        group_ok = (token_index[None, :] <= query_index[:, None]) & (
            token_index < group_len[request]
        )[None, :]
        usable = jnp.concatenate(
            [jnp.broadcast_to(cache_ok[None, :], (group_total, cache_slots)), group_ok], 1
        )[None]
        row_peak = jnp.max(jnp.where(usable, scores, -1e30), -1)
        weights = jnp.where(usable, jnp.exp(scores - row_peak[..., None]), 0.0)
        row_mass = jnp.sum(weights, -1)
        numer_list.append(
            jnp.einsum(
                "hqk,khd->qhd",
                weights.astype(jnp.bfloat16),
                value_rows,
                preferred_element_type=jnp.float32,
            )
        )
        peak_list.append(row_peak.T)
        mass_list.append(row_mass.T)
    numerators = jnp.stack(numer_list)
    row_peaks = jnp.stack(peak_list)
    row_masses = jnp.stack(mass_list)
    seq_count = group_total // local_rows
    numer_width = requests * local_rows * heads_width
    numer_chunks = (
        numerators.reshape(requests, seq_count, local_rows * heads_width)
        .transpose(1, 0, 2)
        .reshape(seq_count, numer_width)
    )
    stats = (
        jnp.stack([row_peaks, row_masses], -1)
        .reshape(requests, seq_count, local_rows * local_heads * 2)
        .transpose(1, 0, 2)
        .reshape(seq_count, -1)
    )
    payload = jnp.concatenate([numer_chunks, stats], -1)
    received = lax.all_to_all(payload, "seq", 0, 0, tiled=True)
    block_numer = received[:, :numer_width].reshape(
        seq_count, requests, local_rows, local_heads, HD
    )
    block_stats = received[:, numer_width:].reshape(
        seq_count, requests, local_rows, local_heads, 2
    )
    block_peak = block_stats[..., 0]
    top_peak = jnp.max(block_peak, 0)
    factor = jnp.exp(block_peak - top_peak)
    numer_sum = jnp.sum(block_numer * factor[..., None], 0)
    mass_sum = jnp.sum(block_stats[..., 1] * factor, 0)
    attended = numer_sum.reshape(requests, local_rows, local_heads, HD) / mass_sum[..., None]
    attended = (
        jnp.where(live_rows[..., None, None], attended, 0.0)
        .astype(jnp.bfloat16)
        .reshape(requests * local_rows, heads_width)
    )
    partial_out = jnp.dot(attended, w_out, preferred_element_type=jnp.float32).reshape(
        requests, local_rows, -1
    )
    mixed = lax.psum_scatter(partial_out, "tensor", scatter_dimension=2, tiled=True).astype(
        jnp.bfloat16
    )
    return (mixed, new_keys, new_values)


def solution(mesh):
    placed = (
        P(None, "seq", "tensor"),
        P(),
        P(None, "tensor"),
        P(None, "tensor"),
        P(None, "tensor"),
        P("tensor", None),
        P(None, "seq", "tensor"),
        P(None, "seq", "tensor"),
        P(),
        P(),
    )
    return jax.shard_map(
        body,
        mesh=mesh,
        in_specs=placed,
        out_specs=(P(None, "seq", "tensor"), P(None, "seq", "tensor"), P(None, "seq", "tensor")),
        check_vma=False,
    )
```

```python
import jax
import jax.numpy as jnp
from jax import lax
from jax.sharding import PartitionSpec as P

HD = 128


def rotate(vector, position):
    half_dim = vector.shape[-1] // 2
    frequency = 1000000.0 ** (-(jnp.arange(half_dim, dtype=jnp.float32) * 2.0 / vector.shape[-1]))
    angles = position.astype(jnp.float32)[..., None] * frequency
    cosine = jnp.concatenate([jnp.cos(angles), jnp.cos(angles)], -1)[..., None, :]
    sine = jnp.concatenate([jnp.sin(angles), jnp.sin(angles)], -1)[..., None, :]
    turned = jnp.concatenate([-vector[..., half_dim:], vector[..., :half_dim]], -1)
    return vector * cosine + turned * sine


def body(
    tokens,
    norm_gain,
    w_query,
    w_key,
    w_value,
    w_out,
    cache_keys,
    cache_values,
    cache_len,
    group_len,
):
    seq_index = lax.axis_index("seq")
    seq_count = lax.axis_size("seq")
    requests, local_rows, width_part = tokens.shape
    heads_width = w_query.shape[1]
    local_heads = heads_width // HD
    cache_slots = cache_keys.shape[1]
    gain = norm_gain.astype(jnp.float32)
    offsets = jnp.arange(local_rows, dtype=jnp.int32)
    token_index = seq_index * local_rows + offsets
    slot_index = seq_index * cache_slots + jnp.arange(cache_slots, dtype=jnp.int32)
    query_index = jnp.arange(seq_count * local_rows, dtype=jnp.int32)
    score_scale = HD ** (-0.5)
    numer_width = local_rows * heads_width
    mixed_list = []
    key_list = []
    value_list = []
    for request in range(requests):
        gathered = lax.all_gather(tokens[request], "tensor", axis=1, tiled=True).astype(
            jnp.float32
        )
        inverse_rms = lax.rsqrt(jnp.mean(gathered * gathered, -1, keepdims=True) + 1e-05)
        normed = (gathered * inverse_rms * gain).astype(jnp.bfloat16)

        def project(weight):
            return jnp.dot(normed, weight, preferred_element_type=jnp.float32).reshape(
                local_rows, local_heads, HD
            )

        position = cache_len[request] + token_index
        queries = rotate(project(w_query)[None], position[None])[0].astype(jnp.bfloat16)
        key_new = rotate(project(w_key)[None], position[None])[0].astype(jnp.bfloat16)
        value_new = project(w_value).astype(jnp.bfloat16)
        live_rows = token_index < group_len[request]
        key_list.append(
            jnp.where(live_rows[:, None], key_new.reshape(local_rows, heads_width), 0.0).astype(
                jnp.bfloat16
            )
        )
        value_list.append(
            jnp.where(live_rows[:, None], value_new.reshape(local_rows, heads_width), 0.0).astype(
                jnp.bfloat16
            )
        )
        all_queries = lax.all_gather(queries, "seq", axis=0, tiled=True)
        cache_k = cache_keys[request].reshape(cache_slots, local_heads, HD)
        cache_v = cache_values[request].reshape(cache_slots, local_heads, HD)
        cache_ok = (slot_index < cache_len[request])[None, None, :]
        group_ok = ((token_index[None, :] <= query_index[:, None]) & live_rows[None, :])[None]
        cache_scores = jnp.where(
            cache_ok,
            jnp.einsum("qhd,khd->hqk", all_queries, cache_k, preferred_element_type=jnp.float32)
            * score_scale,
            -1e30,
        )
        group_scores = jnp.where(
            group_ok,
            jnp.einsum("qhd,khd->hqk", all_queries, key_new, preferred_element_type=jnp.float32)
            * score_scale,
            -1e30,
        )
        row_peak = jnp.maximum(jnp.max(cache_scores, -1), jnp.max(group_scores, -1))
        cache_weights = jnp.where(cache_ok, jnp.exp(cache_scores - row_peak[..., None]), 0.0)
        group_weights = jnp.where(group_ok, jnp.exp(group_scores - row_peak[..., None]), 0.0)
        row_mass = jnp.sum(cache_weights, -1) + jnp.sum(group_weights, -1)
        numerators = jnp.einsum(
            "hqk,khd->qhd",
            cache_weights.astype(jnp.bfloat16),
            cache_v,
            preferred_element_type=jnp.float32,
        ) + jnp.einsum(
            "hqk,khd->qhd",
            group_weights.astype(jnp.bfloat16),
            value_new,
            preferred_element_type=jnp.float32,
        )
        stats = jnp.stack([row_peak.T, row_mass.T], -1)
        payload = jnp.concatenate(
            [
                numerators.reshape(seq_count, numer_width),
                stats.reshape(seq_count, local_rows * local_heads * 2),
            ],
            -1,
        )
        received = lax.all_to_all(payload, "seq", 0, 0, tiled=True)
        block_numer = received[:, :numer_width].reshape(seq_count, local_rows, local_heads, HD)
        block_stats = received[:, numer_width:].reshape(seq_count, local_rows, local_heads, 2)
        block_peak = block_stats[..., 0]
        factor = jnp.exp(block_peak - jnp.max(block_peak, 0))
        numer_sum = jnp.sum(block_numer * factor[..., None], 0)
        mass_sum = jnp.sum(block_stats[..., 1] * factor, 0)
        attended = numer_sum / mass_sum[..., None]
        attended = (
            jnp.where(live_rows[:, None, None], attended, 0.0)
            .astype(jnp.bfloat16)
            .reshape(local_rows, heads_width)
        )
        partial_out = jnp.dot(attended, w_out, preferred_element_type=jnp.float32)
        mixed_list.append(
            lax.psum_scatter(partial_out, "tensor", scatter_dimension=1, tiled=True).astype(
                jnp.bfloat16
            )
        )
    return (jnp.stack(mixed_list), jnp.stack(key_list), jnp.stack(value_list))


def solution(mesh):
    placed = (
        P(None, "seq", "tensor"),
        P(),
        P(None, "tensor"),
        P(None, "tensor"),
        P(None, "tensor"),
        P("tensor", None),
        P(None, "seq", "tensor"),
        P(None, "seq", "tensor"),
        P(),
        P(),
    )
    return jax.shard_map(
        body,
        mesh=mesh,
        in_specs=placed,
        out_specs=(P(None, "seq", "tensor"), P(None, "seq", "tensor"), P(None, "seq", "tensor")),
        check_vma=False,
    )
```

```python
import jax
import jax.numpy as jnp
from jax import lax
from jax.sharding import PartitionSpec as P

HD = 128


def rotate(vector, position):
    half_dim = vector.shape[-1] // 2
    frequency = 1000000.0 ** (-(jnp.arange(half_dim, dtype=jnp.float32) * 2.0 / vector.shape[-1]))
    angles = position.astype(jnp.float32)[..., None] * frequency
    cosine = jnp.concatenate([jnp.cos(angles), jnp.cos(angles)], -1)[..., None, :]
    sine = jnp.concatenate([jnp.sin(angles), jnp.sin(angles)], -1)[..., None, :]
    turned = jnp.concatenate([-vector[..., half_dim:], vector[..., :half_dim]], -1)
    return vector * cosine + turned * sine


def body(
    tokens,
    norm_gain,
    w_query,
    w_key,
    w_value,
    w_out,
    cache_keys,
    cache_values,
    cache_len,
    group_len,
):
    seq_index = lax.axis_index("seq")
    requests, local_rows, width_part = tokens.shape
    gathered = lax.all_gather(tokens, "tensor", axis=2, tiled=True).astype(jnp.float32)
    inverse_rms = lax.rsqrt(jnp.mean(gathered * gathered, -1, keepdims=True) + 1e-05)
    normed = (gathered * inverse_rms * norm_gain.astype(jnp.float32)).astype(jnp.bfloat16)
    flat_rows = normed.reshape(requests * local_rows, -1)
    heads_width = w_query.shape[1]
    local_heads = heads_width // HD

    def project(weight):
        return jnp.dot(flat_rows, weight, preferred_element_type=jnp.float32).reshape(
            requests, local_rows, local_heads, HD
        )

    offsets = jnp.arange(local_rows, dtype=jnp.int32)
    first_row = seq_index * local_rows
    position = cache_len[:, None] + first_row + offsets[None, :]
    queries = (
        rotate(project(w_query), position)
        .astype(jnp.bfloat16)
        .reshape(requests, local_rows, heads_width)
    )
    key_new = (
        rotate(project(w_key), position)
        .astype(jnp.bfloat16)
        .reshape(requests, local_rows, heads_width)
    )
    value_new = project(w_value).astype(jnp.bfloat16).reshape(requests, local_rows, heads_width)
    live_rows = (first_row + offsets)[None, :] < group_len[:, None]
    new_keys = jnp.where(live_rows[..., None], key_new, jnp.zeros_like(key_new))
    new_values = jnp.where(live_rows[..., None], value_new, jnp.zeros_like(value_new))
    all_queries = lax.all_gather(queries, "seq", axis=1, tiled=True)
    group_total = all_queries.shape[1]
    seq_count = group_total // local_rows
    cache_slots = cache_keys.shape[1]
    slot_index = seq_index * cache_slots + jnp.arange(cache_slots, dtype=jnp.int32)
    query_index = jnp.arange(group_total, dtype=jnp.int32)
    token_index = first_row + offsets
    score_scale = HD ** (-0.5)
    numer_width = local_rows * heads_width
    attended_list = []
    for request in range(requests):
        query_rows = all_queries[request].reshape(group_total, local_heads, HD)
        cache_k = cache_keys[request].reshape(cache_slots, local_heads, HD)
        cache_v = cache_values[request].reshape(cache_slots, local_heads, HD)
        group_k = key_new[request].reshape(local_rows, local_heads, HD)
        group_v = value_new[request].reshape(local_rows, local_heads, HD)
        cache_ok = (slot_index < cache_len[request])[None, None, :]
        group_ok = (
            (token_index[None, :] <= query_index[:, None])
            & (token_index < group_len[request])[None, :]
        )[None]
        cache_scores = jnp.where(
            cache_ok,
            jnp.einsum("qhd,khd->hqk", query_rows, cache_k, preferred_element_type=jnp.float32)
            * score_scale,
            -1e30,
        )
        group_scores = jnp.where(
            group_ok,
            jnp.einsum("qhd,khd->hqk", query_rows, group_k, preferred_element_type=jnp.float32)
            * score_scale,
            -1e30,
        )
        row_peak = jnp.maximum(jnp.max(cache_scores, -1), jnp.max(group_scores, -1))
        cache_weights = jnp.where(cache_ok, jnp.exp(cache_scores - row_peak[..., None]), 0.0)
        group_weights = jnp.where(group_ok, jnp.exp(group_scores - row_peak[..., None]), 0.0)
        row_mass = jnp.sum(cache_weights, -1) + jnp.sum(group_weights, -1)
        numerators = jnp.einsum(
            "hqk,khd->qhd",
            cache_weights.astype(jnp.bfloat16),
            cache_v,
            preferred_element_type=jnp.float32,
        ) + jnp.einsum(
            "hqk,khd->qhd",
            group_weights.astype(jnp.bfloat16),
            group_v,
            preferred_element_type=jnp.float32,
        )
        stats = jnp.stack([row_peak.T, row_mass.T], -1)
        payload = jnp.concatenate(
            [
                numerators.reshape(seq_count, numer_width),
                stats.reshape(seq_count, local_rows * local_heads * 2),
            ],
            -1,
        )
        received = lax.all_to_all(payload, "seq", 0, 0, tiled=True)
        block_numer = received[:, :numer_width].reshape(seq_count, local_rows, local_heads, HD)
        block_stats = received[:, numer_width:].reshape(seq_count, local_rows, local_heads, 2)
        block_peak = block_stats[..., 0]
        factor = jnp.exp(block_peak - jnp.max(block_peak, 0))
        numer_sum = jnp.sum(block_numer * factor[..., None], 0)
        mass_sum = jnp.sum(block_stats[..., 1] * factor, 0)
        attended_list.append(numer_sum / mass_sum[..., None])
    attended = (
        jnp.where(live_rows[..., None, None], jnp.stack(attended_list), 0.0)
        .astype(jnp.bfloat16)
        .reshape(requests * local_rows, heads_width)
    )
    partial_out = jnp.dot(attended, w_out, preferred_element_type=jnp.float32).reshape(
        requests, local_rows, -1
    )
    mixed = lax.psum_scatter(partial_out, "tensor", scatter_dimension=2, tiled=True).astype(
        jnp.bfloat16
    )
    return (mixed, new_keys, new_values)


def solution(mesh):
    placed = (
        P(None, "seq", "tensor"),
        P(),
        P(None, "tensor"),
        P(None, "tensor"),
        P(None, "tensor"),
        P("tensor", None),
        P(None, "seq", "tensor"),
        P(None, "seq", "tensor"),
        P(),
        P(),
    )
    return jax.shard_map(
        body,
        mesh=mesh,
        in_specs=placed,
        out_specs=(P(None, "seq", "tensor"), P(None, "seq", "tensor"), P(None, "seq", "tensor")),
        check_vma=False,
    )
```

```python
import jax
import jax.numpy as jnp
from jax import lax
from jax.sharding import PartitionSpec as P

HD = 128


def rotate(vector, position):
    half_dim = vector.shape[-1] // 2
    frequency = 1000000.0 ** (-(jnp.arange(half_dim, dtype=jnp.float32) * 2.0 / vector.shape[-1]))
    angles = position.astype(jnp.float32)[..., None] * frequency
    cosine = jnp.concatenate([jnp.cos(angles), jnp.cos(angles)], -1)[..., None, :]
    sine = jnp.concatenate([jnp.sin(angles), jnp.sin(angles)], -1)[..., None, :]
    turned = jnp.concatenate([-vector[..., half_dim:], vector[..., :half_dim]], -1)
    return vector * cosine + turned * sine


def body(
    tokens,
    norm_gain,
    w_query,
    w_key,
    w_value,
    w_out,
    cache_keys,
    cache_values,
    cache_len,
    group_len,
):
    seq_index = lax.axis_index("seq")
    requests, local_rows, width_part = tokens.shape
    gathered = lax.all_gather(tokens, "tensor", axis=2, tiled=True).astype(jnp.float32)
    inverse_rms = lax.rsqrt(jnp.mean(gathered * gathered, -1, keepdims=True) + 1e-05)
    normed = (gathered * inverse_rms * norm_gain.astype(jnp.float32)).astype(jnp.bfloat16)
    flat_rows = normed.reshape(requests * local_rows, -1)
    heads_width = w_query.shape[1]
    local_heads = heads_width // HD

    def project(weight):
        return jnp.dot(flat_rows, weight, preferred_element_type=jnp.float32).reshape(
            requests, local_rows, local_heads, HD
        )

    offsets = jnp.arange(local_rows, dtype=jnp.int32)
    first_row = seq_index * local_rows
    position = cache_len[:, None] + first_row + offsets[None, :]
    queries = (
        rotate(project(w_query), position)
        .astype(jnp.bfloat16)
        .reshape(requests, local_rows, heads_width)
    )
    key_new = (
        rotate(project(w_key), position)
        .astype(jnp.bfloat16)
        .reshape(requests, local_rows, heads_width)
    )
    value_new = project(w_value).astype(jnp.bfloat16).reshape(requests, local_rows, heads_width)
    live_rows = (first_row + offsets)[None, :] < group_len[:, None]
    new_keys = jnp.where(live_rows[..., None], key_new, jnp.zeros_like(key_new))
    new_values = jnp.where(live_rows[..., None], value_new, jnp.zeros_like(value_new))
    seq_count = lax.axis_size("seq")
    tensor_count = lax.axis_size("tensor")
    group_total = seq_count * local_rows
    cache_slots = cache_keys.shape[1]
    slot_index = seq_index * cache_slots + jnp.arange(cache_slots, dtype=jnp.int32)
    query_index = jnp.arange(group_total, dtype=jnp.int32)
    token_index = first_row + offsets
    score_scale = HD ** (-0.5)
    numer_width = local_rows * heads_width
    mixed_list = []
    for request in range(requests):
        query_copies = jnp.broadcast_to(queries[request][None], (seq_count, local_rows, heads_width))
        query_rows = lax.all_to_all(query_copies, "seq", 0, 0, tiled=True).reshape(
            group_total, local_heads, HD
        )
        cache_k = cache_keys[request].reshape(cache_slots, local_heads, HD)
        cache_v = cache_values[request].reshape(cache_slots, local_heads, HD)
        group_k = key_new[request].reshape(local_rows, local_heads, HD)
        group_v = value_new[request].reshape(local_rows, local_heads, HD)
        cache_ok = (slot_index < cache_len[request])[None, None, :]
        group_ok = (
            (token_index[None, :] <= query_index[:, None])
            & (token_index < group_len[request])[None, :]
        )[None]
        cache_scores = jnp.where(
            cache_ok,
            jnp.einsum("qhd,khd->hqk", query_rows, cache_k, preferred_element_type=jnp.float32)
            * score_scale,
            -1e30,
        )
        group_scores = jnp.where(
            group_ok,
            jnp.einsum("qhd,khd->hqk", query_rows, group_k, preferred_element_type=jnp.float32)
            * score_scale,
            -1e30,
        )
        row_peak = jnp.maximum(jnp.max(cache_scores, -1), jnp.max(group_scores, -1))
        cache_weights = jnp.where(cache_ok, jnp.exp(cache_scores - row_peak[..., None]), 0.0)
        group_weights = jnp.where(group_ok, jnp.exp(group_scores - row_peak[..., None]), 0.0)
        row_mass = jnp.sum(cache_weights, -1) + jnp.sum(group_weights, -1)
        numerators = jnp.einsum(
            "hqk,khd->qhd",
            cache_weights.astype(jnp.bfloat16),
            cache_v,
            preferred_element_type=jnp.float32,
        ) + jnp.einsum(
            "hqk,khd->qhd",
            group_weights.astype(jnp.bfloat16),
            group_v,
            preferred_element_type=jnp.float32,
        )
        stats = jnp.stack([row_peak.T, row_mass.T], -1)
        payload = jnp.concatenate(
            [
                numerators.reshape(seq_count, numer_width),
                stats.reshape(seq_count, local_rows * local_heads * 2),
            ],
            -1,
        )
        received = lax.all_to_all(payload, "seq", 0, 0, tiled=True)
        block_numer = received[:, :numer_width].reshape(seq_count, local_rows, local_heads, HD)
        block_stats = received[:, numer_width:].reshape(seq_count, local_rows, local_heads, 2)
        block_peak = block_stats[..., 0]
        factor = jnp.exp(block_peak - jnp.max(block_peak, 0))
        numer_sum = jnp.sum(block_numer * factor[..., None], 0)
        mass_sum = jnp.sum(block_stats[..., 1] * factor, 0)
        attended = (
            jnp.where(live_rows[request][:, None, None], numer_sum / mass_sum[..., None], 0.0)
            .astype(jnp.bfloat16)
            .reshape(local_rows, heads_width)
        )
        partial_out = jnp.einsum(
            "rk,kcn->crn",
            attended,
            w_out.reshape(heads_width, tensor_count, -1),
            preferred_element_type=jnp.float32,
        )
        partial_sums = lax.all_to_all(partial_out, "tensor", 0, 0, tiled=True)
        mixed_list.append(jnp.sum(partial_sums, 0).astype(jnp.bfloat16))
    mixed = jnp.stack(mixed_list)
    return (mixed, new_keys, new_values)


def solution(mesh):
    placed = (
        P(None, "seq", "tensor"),
        P(),
        P(None, "tensor"),
        P(None, "tensor"),
        P(None, "tensor"),
        P("tensor", None),
        P(None, "seq", "tensor"),
        P(None, "seq", "tensor"),
        P(),
        P(),
    )
    return jax.shard_map(
        body,
        mesh=mesh,
        in_specs=placed,
        out_specs=(P(None, "seq", "tensor"), P(None, "seq", "tensor"), P(None, "seq", "tensor")),
        check_vma=False,
    )
```

```python
import jax
import jax.numpy as jnp
from jax import lax
from jax.sharding import PartitionSpec as P

HD = 128


def rotate(vector, position):
    half_dim = vector.shape[-1] // 2
    frequency = 1000000.0 ** (-(jnp.arange(half_dim, dtype=jnp.float32) * 2.0 / vector.shape[-1]))
    angles = position.astype(jnp.float32)[..., None] * frequency
    cosine = jnp.concatenate([jnp.cos(angles), jnp.cos(angles)], -1)[..., None, :]
    sine = jnp.concatenate([jnp.sin(angles), jnp.sin(angles)], -1)[..., None, :]
    turned = jnp.concatenate([-vector[..., half_dim:], vector[..., :half_dim]], -1)
    return vector * cosine + turned * sine


def body(
    tokens,
    norm_gain,
    w_query,
    w_key,
    w_value,
    w_out,
    cache_keys,
    cache_values,
    cache_len,
    group_len,
):
    seq_index = lax.axis_index("seq")
    requests, local_rows, width_part = tokens.shape
    gathered = lax.all_gather(tokens, "tensor", axis=2, tiled=True).astype(jnp.float32)
    inverse_rms = lax.rsqrt(jnp.mean(gathered * gathered, -1, keepdims=True) + 1e-05)
    normed = (gathered * inverse_rms * norm_gain.astype(jnp.float32)).astype(jnp.bfloat16)
    flat_rows = normed.reshape(requests * local_rows, -1)
    heads_width = w_query.shape[1]
    local_heads = heads_width // HD

    def project(weight):
        return jnp.dot(flat_rows, weight, preferred_element_type=jnp.float32).reshape(
            requests, local_rows, local_heads, HD
        )

    offsets = jnp.arange(local_rows, dtype=jnp.int32)
    first_row = seq_index * local_rows
    position = cache_len[:, None] + first_row + offsets[None, :]
    queries = (
        rotate(project(w_query), position)
        .astype(jnp.bfloat16)
        .reshape(requests, local_rows, heads_width)
    )
    key_new = (
        rotate(project(w_key), position)
        .astype(jnp.bfloat16)
        .reshape(requests, local_rows, heads_width)
    )
    value_new = project(w_value).astype(jnp.bfloat16).reshape(requests, local_rows, heads_width)
    live_rows = (first_row + offsets)[None, :] < group_len[:, None]
    new_keys = jnp.where(live_rows[..., None], key_new, jnp.zeros_like(key_new))
    new_values = jnp.where(live_rows[..., None], value_new, jnp.zeros_like(value_new))
    all_queries = lax.all_gather(queries, "seq", axis=1, tiled=True)
    group_total = all_queries.shape[1]
    seq_count = group_total // local_rows
    cache_slots = cache_keys.shape[1]
    slot_index = seq_index * cache_slots + jnp.arange(cache_slots, dtype=jnp.int32)
    query_index = jnp.arange(group_total, dtype=jnp.int32)
    token_index = first_row + offsets
    score_scale = HD ** (-0.5)
    numer_width = local_rows * heads_width
    attended_list = []
    for request in range(requests):
        query_rows = all_queries[request].reshape(group_total, local_heads, HD)
        cache_k = cache_keys[request].reshape(cache_slots, local_heads, HD)
        cache_v = cache_values[request].reshape(cache_slots, local_heads, HD)
        group_k = key_new[request].reshape(local_rows, local_heads, HD)
        group_v = value_new[request].reshape(local_rows, local_heads, HD)
        cache_ok = (slot_index < cache_len[request])[None, None, :]
        group_ok = (
            (token_index[None, :] <= query_index[:, None])
            & (token_index < group_len[request])[None, :]
        )[None]
        cache_scores = jnp.where(
            cache_ok,
            jnp.einsum("qhd,khd->hqk", query_rows, cache_k, preferred_element_type=jnp.float32)
            * score_scale,
            -1e30,
        )
        group_scores = jnp.where(
            group_ok,
            jnp.einsum("qhd,khd->hqk", query_rows, group_k, preferred_element_type=jnp.float32)
            * score_scale,
            -1e30,
        )
        row_peak = jnp.maximum(jnp.max(cache_scores, -1), jnp.max(group_scores, -1))
        cache_weights = jnp.where(cache_ok, jnp.exp(cache_scores - row_peak[..., None]), 0.0)
        group_weights = jnp.where(group_ok, jnp.exp(group_scores - row_peak[..., None]), 0.0)
        row_mass = jnp.sum(cache_weights, -1) + jnp.sum(group_weights, -1)
        numerators = jnp.einsum(
            "hqk,khd->qhd",
            cache_weights.astype(jnp.bfloat16),
            cache_v,
            preferred_element_type=jnp.float32,
        ) + jnp.einsum(
            "hqk,khd->qhd",
            group_weights.astype(jnp.bfloat16),
            group_v,
            preferred_element_type=jnp.float32,
        )
        stats = jnp.stack([row_peak.T, row_mass.T], -1)
        pair_rows = local_rows * local_heads
        payload = jnp.concatenate(
            [
                numerators.reshape(seq_count, pair_rows, HD),
                stats.reshape(seq_count, -1, HD),
            ],
            1,
        )
        received = lax.all_to_all(payload, "seq", 0, 0, tiled=True)
        block_stats = received[:, pair_rows:].reshape(seq_count, pair_rows, 2)
        block_peak = block_stats[..., 0]
        factor = jnp.exp(block_peak - jnp.max(block_peak, 0))
        mass_sum = jnp.sum(block_stats[..., 1] * factor, 0).reshape(local_rows, local_heads)
        numer_sum = jnp.sum(received[:, :pair_rows] * factor[..., None], 0)
        numer_sum = numer_sum.reshape(local_rows, local_heads, HD)
        attended_list.append(numer_sum / mass_sum[..., None])
    attended = (
        jnp.where(live_rows[..., None, None], jnp.stack(attended_list), 0.0)
        .astype(jnp.bfloat16)
        .reshape(requests * local_rows, heads_width)
    )
    partial_out = jnp.dot(attended, w_out, preferred_element_type=jnp.float32).reshape(
        requests, local_rows, -1
    )
    mixed = lax.psum_scatter(partial_out, "tensor", scatter_dimension=2, tiled=True).astype(
        jnp.bfloat16
    )
    return (mixed, new_keys, new_values)


def solution(mesh):
    placed = (
        P(None, "seq", "tensor"),
        P(),
        P(None, "tensor"),
        P(None, "tensor"),
        P(None, "tensor"),
        P("tensor", None),
        P(None, "seq", "tensor"),
        P(None, "seq", "tensor"),
        P(),
        P(),
    )
    return jax.shard_map(
        body,
        mesh=mesh,
        in_specs=placed,
        out_specs=(P(None, "seq", "tensor"), P(None, "seq", "tensor"), P(None, "seq", "tensor")),
        check_vma=False,
    )
```

```python
import jax
import jax.numpy as jnp
from jax import lax
from jax.sharding import PartitionSpec as P

HD = 128


def rotate(vector, position):
    half_dim = vector.shape[-1] // 2
    frequency = 1000000.0 ** (-(jnp.arange(half_dim, dtype=jnp.float32) * 2.0 / vector.shape[-1]))
    angles = position.astype(jnp.float32)[..., None] * frequency
    cosine = jnp.concatenate([jnp.cos(angles), jnp.cos(angles)], -1)[..., None, :]
    sine = jnp.concatenate([jnp.sin(angles), jnp.sin(angles)], -1)[..., None, :]
    turned = jnp.concatenate([-vector[..., half_dim:], vector[..., :half_dim]], -1)
    return vector * cosine + turned * sine


def body(
    tokens,
    norm_gain,
    w_query,
    w_key,
    w_value,
    w_out,
    cache_keys,
    cache_values,
    cache_len,
    group_len,
):
    seq_index = lax.axis_index("seq")
    requests, local_rows, width_part = tokens.shape
    gathered = lax.all_gather(tokens, "tensor", axis=2, tiled=True).astype(jnp.float32)
    inverse_rms = lax.rsqrt(jnp.mean(gathered * gathered, -1, keepdims=True) + 1e-05)
    normed = (gathered * inverse_rms * norm_gain.astype(jnp.float32)).astype(jnp.bfloat16)
    flat_rows = normed.reshape(requests * local_rows, -1)
    heads_width = w_query.shape[1]
    local_heads = heads_width // HD

    def project(weight):
        return jnp.dot(flat_rows, weight, preferred_element_type=jnp.float32).reshape(
            requests, local_rows, local_heads, HD
        )

    offsets = jnp.arange(local_rows, dtype=jnp.int32)
    first_row = seq_index * local_rows
    position = cache_len[:, None] + first_row + offsets[None, :]
    queries = (
        rotate(project(w_query), position)
        .astype(jnp.bfloat16)
        .reshape(requests, local_rows, heads_width)
    )
    key_new = (
        rotate(project(w_key), position)
        .astype(jnp.bfloat16)
        .reshape(requests, local_rows, heads_width)
    )
    value_new = project(w_value).astype(jnp.bfloat16).reshape(requests, local_rows, heads_width)
    live_rows = (first_row + offsets)[None, :] < group_len[:, None]
    new_keys = jnp.where(live_rows[..., None], key_new, jnp.zeros_like(key_new))
    new_values = jnp.where(live_rows[..., None], value_new, jnp.zeros_like(value_new))
    all_queries = lax.all_gather(queries, "seq", axis=1, tiled=True)
    group_total = all_queries.shape[1]
    seq_count = group_total // local_rows
    cache_slots = cache_keys.shape[1]
    slot_index = seq_index * cache_slots + jnp.arange(cache_slots, dtype=jnp.int32)
    query_index = jnp.arange(group_total, dtype=jnp.int32)
    token_index = first_row + offsets
    score_scale = HD ** (-0.5)
    numer_width = local_rows * heads_width
    attended_list = []
    payload_list = []
    for request in range(requests):
        query_rows = all_queries[request].reshape(group_total, local_heads, HD)
        cache_k = cache_keys[request].reshape(cache_slots, local_heads, HD)
        cache_v = cache_values[request].reshape(cache_slots, local_heads, HD)
        group_k = key_new[request].reshape(local_rows, local_heads, HD)
        group_v = value_new[request].reshape(local_rows, local_heads, HD)
        cache_ok = (slot_index < cache_len[request])[None, None, :]
        group_ok = (
            (token_index[None, :] <= query_index[:, None])
            & (token_index < group_len[request])[None, :]
        )[None]
        cache_scores = jnp.where(
            cache_ok,
            jnp.einsum("qhd,khd->hqk", query_rows, cache_k, preferred_element_type=jnp.float32)
            * score_scale,
            -1e30,
        )
        group_scores = jnp.where(
            group_ok,
            jnp.einsum("qhd,khd->hqk", query_rows, group_k, preferred_element_type=jnp.float32)
            * score_scale,
            -1e30,
        )
        row_peak = jnp.maximum(jnp.max(cache_scores, -1), jnp.max(group_scores, -1))
        cache_weights = jnp.where(cache_ok, jnp.exp(cache_scores - row_peak[..., None]), 0.0)
        group_weights = jnp.where(group_ok, jnp.exp(group_scores - row_peak[..., None]), 0.0)
        row_mass = jnp.sum(cache_weights, -1) + jnp.sum(group_weights, -1)
        numerators = jnp.einsum(
            "hqk,khd->qhd",
            cache_weights.astype(jnp.bfloat16),
            cache_v,
            preferred_element_type=jnp.float32,
        ) + jnp.einsum(
            "hqk,khd->qhd",
            group_weights.astype(jnp.bfloat16),
            group_v,
            preferred_element_type=jnp.float32,
        )
        stats = jnp.stack([row_peak.T, row_mass.T], -1)
        pair_rows = local_rows * local_heads
        payload = jnp.concatenate(
            [
                numerators.reshape(seq_count, pair_rows, HD),
                stats.reshape(seq_count, -1, HD),
            ],
            1,
        )
        payload_list.append(payload)
    block_rows = payload_list[0].shape[1]
    for first in range(0, requests, 2):
        sent = jnp.concatenate(payload_list[first : first + 2], 1)
        arrived = lax.all_to_all(sent, "seq", 0, 0, tiled=True)
        for member in range(sent.shape[1] // block_rows):
            received = arrived[:, member * block_rows : (member + 1) * block_rows]
            block_stats = received[:, pair_rows:].reshape(seq_count, pair_rows, 2)
            block_peak = block_stats[..., 0]
            factor = jnp.exp(block_peak - jnp.max(block_peak, 0))
            mass_sum = jnp.sum(block_stats[..., 1] * factor, 0).reshape(local_rows, local_heads)
            numer_sum = jnp.sum(received[:, :pair_rows] * factor[..., None], 0)
            numer_sum = numer_sum.reshape(local_rows, local_heads, HD)
            attended_list.append(numer_sum / mass_sum[..., None])
    attended = (
        jnp.where(live_rows[..., None, None], jnp.stack(attended_list), 0.0)
        .astype(jnp.bfloat16)
        .reshape(requests * local_rows, heads_width)
    )
    partial_out = jnp.dot(attended, w_out, preferred_element_type=jnp.float32).reshape(
        requests, local_rows, -1
    )
    mixed = lax.psum_scatter(partial_out, "tensor", scatter_dimension=2, tiled=True).astype(
        jnp.bfloat16
    )
    return (mixed, new_keys, new_values)


def solution(mesh):
    placed = (
        P(None, "seq", "tensor"),
        P(),
        P(None, "tensor"),
        P(None, "tensor"),
        P(None, "tensor"),
        P("tensor", None),
        P(None, "seq", "tensor"),
        P(None, "seq", "tensor"),
        P(),
        P(),
    )
    return jax.shard_map(
        body,
        mesh=mesh,
        in_specs=placed,
        out_specs=(P(None, "seq", "tensor"), P(None, "seq", "tensor"), P(None, "seq", "tensor")),
        check_vma=False,
    )
```

```python
import jax
import jax.numpy as jnp
from jax import lax
from jax.sharding import PartitionSpec as P

HD = 128


def rotate(vector, position):
    half_dim = vector.shape[-1] // 2
    frequency = 1000000.0 ** (-(jnp.arange(half_dim, dtype=jnp.float32) * 2.0 / vector.shape[-1]))
    angles = position.astype(jnp.float32)[..., None] * frequency
    cosine = jnp.concatenate([jnp.cos(angles), jnp.cos(angles)], -1)[..., None, :]
    sine = jnp.concatenate([jnp.sin(angles), jnp.sin(angles)], -1)[..., None, :]
    turned = jnp.concatenate([-vector[..., half_dim:], vector[..., :half_dim]], -1)
    return vector * cosine + turned * sine


def body(
    tokens,
    norm_gain,
    w_query,
    w_key,
    w_value,
    w_out,
    cache_keys,
    cache_values,
    cache_len,
    group_len,
):
    seq_index = lax.axis_index("seq")
    requests, local_rows, width_part = tokens.shape
    gathered = lax.all_gather(tokens, "tensor", axis=2, tiled=True).astype(jnp.float32)
    inverse_rms = lax.rsqrt(jnp.mean(gathered * gathered, -1, keepdims=True) + 1e-05)
    normed = (gathered * inverse_rms * norm_gain.astype(jnp.float32)).astype(jnp.bfloat16)
    flat_rows = normed.reshape(requests * local_rows, -1)
    heads_width = w_query.shape[1]
    local_heads = heads_width // HD

    def project(weight):
        return jnp.dot(flat_rows, weight, preferred_element_type=jnp.float32).reshape(
            requests, local_rows, local_heads, HD
        )

    offsets = jnp.arange(local_rows, dtype=jnp.int32)
    first_row = seq_index * local_rows
    position = cache_len[:, None] + first_row + offsets[None, :]
    queries = (
        rotate(project(w_query), position)
        .astype(jnp.bfloat16)
        .reshape(requests, local_rows, heads_width)
    )
    key_new = (
        rotate(project(w_key), position)
        .astype(jnp.bfloat16)
        .reshape(requests, local_rows, heads_width)
    )
    value_new = project(w_value).astype(jnp.bfloat16).reshape(requests, local_rows, heads_width)
    live_rows = (first_row + offsets)[None, :] < group_len[:, None]
    new_keys = jnp.where(live_rows[..., None], key_new, jnp.zeros_like(key_new))
    new_values = jnp.where(live_rows[..., None], value_new, jnp.zeros_like(value_new))
    pair_queries = [
        lax.all_gather(queries[first : first + 2], "seq", axis=1, tiled=True)
        for first in range(0, requests, 2)
    ]
    group_total = pair_queries[0].shape[1]
    seq_count = group_total // local_rows
    cache_slots = cache_keys.shape[1]
    slot_index = seq_index * cache_slots + jnp.arange(cache_slots, dtype=jnp.int32)
    query_index = jnp.arange(group_total, dtype=jnp.int32)
    token_index = first_row + offsets
    score_scale = HD ** (-0.5)
    numer_width = local_rows * heads_width
    attended_list = []
    payload_list = []
    for request in range(requests):
        query_rows = pair_queries[request // 2][request % 2].reshape(group_total, local_heads, HD)
        cache_k = cache_keys[request].reshape(cache_slots, local_heads, HD)
        cache_v = cache_values[request].reshape(cache_slots, local_heads, HD)
        group_k = key_new[request].reshape(local_rows, local_heads, HD)
        group_v = value_new[request].reshape(local_rows, local_heads, HD)
        cache_ok = (slot_index < cache_len[request])[None, None, :]
        group_ok = (
            (token_index[None, :] <= query_index[:, None])
            & (token_index < group_len[request])[None, :]
        )[None]
        cache_scores = jnp.where(
            cache_ok,
            jnp.einsum("qhd,khd->hqk", query_rows, cache_k, preferred_element_type=jnp.float32)
            * score_scale,
            -1e30,
        )
        group_scores = jnp.where(
            group_ok,
            jnp.einsum("qhd,khd->hqk", query_rows, group_k, preferred_element_type=jnp.float32)
            * score_scale,
            -1e30,
        )
        row_peak = jnp.maximum(jnp.max(cache_scores, -1), jnp.max(group_scores, -1))
        cache_weights = jnp.where(cache_ok, jnp.exp(cache_scores - row_peak[..., None]), 0.0)
        group_weights = jnp.where(group_ok, jnp.exp(group_scores - row_peak[..., None]), 0.0)
        row_mass = jnp.sum(cache_weights, -1) + jnp.sum(group_weights, -1)
        numerators = jnp.einsum(
            "hqk,khd->qhd",
            cache_weights.astype(jnp.bfloat16),
            cache_v,
            preferred_element_type=jnp.float32,
        ) + jnp.einsum(
            "hqk,khd->qhd",
            group_weights.astype(jnp.bfloat16),
            group_v,
            preferred_element_type=jnp.float32,
        )
        stats = jnp.stack([row_peak.T, row_mass.T], -1)
        pair_rows = local_rows * local_heads
        payload = jnp.concatenate(
            [
                numerators.reshape(seq_count, pair_rows, HD),
                stats.reshape(seq_count, -1, HD),
            ],
            1,
        )
        payload_list.append(payload)
    block_rows = payload_list[0].shape[1]
    for first in range(0, requests, 2):
        sent = jnp.concatenate(payload_list[first : first + 2], 1)
        arrived = lax.all_to_all(sent, "seq", 0, 0, tiled=True)
        for member in range(sent.shape[1] // block_rows):
            received = arrived[:, member * block_rows : (member + 1) * block_rows]
            block_stats = received[:, pair_rows:].reshape(seq_count, pair_rows, 2)
            block_peak = block_stats[..., 0]
            factor = jnp.exp(block_peak - jnp.max(block_peak, 0))
            mass_sum = jnp.sum(block_stats[..., 1] * factor, 0).reshape(local_rows, local_heads)
            numer_sum = jnp.sum(received[:, :pair_rows] * factor[..., None], 0)
            numer_sum = numer_sum.reshape(local_rows, local_heads, HD)
            attended_list.append(numer_sum / mass_sum[..., None])
    mixed_list = []
    for first in range(0, requests, 2):
        attended = (
            jnp.where(
                live_rows[first : first + 2, :, None, None],
                jnp.stack(attended_list[first : first + 2]),
                0.0,
            )
            .astype(jnp.bfloat16)
            .reshape(-1, heads_width)
        )
        partial_out = jnp.dot(attended, w_out, preferred_element_type=jnp.float32).reshape(
            -1, local_rows, w_out.shape[1]
        )
        mixed_list.append(
            lax.psum_scatter(partial_out, "tensor", scatter_dimension=2, tiled=True).astype(
                jnp.bfloat16
            )
        )
    mixed = jnp.concatenate(mixed_list, 0)
    return (mixed, new_keys, new_values)


def solution(mesh):
    placed = (
        P(None, "seq", "tensor"),
        P(),
        P(None, "tensor"),
        P(None, "tensor"),
        P(None, "tensor"),
        P("tensor", None),
        P(None, "seq", "tensor"),
        P(None, "seq", "tensor"),
        P(),
        P(),
    )
    return jax.shard_map(
        body,
        mesh=mesh,
        in_specs=placed,
        out_specs=(P(None, "seq", "tensor"), P(None, "seq", "tensor"), P(None, "seq", "tensor")),
        check_vma=False,
    )
```

```python
import jax
import jax.numpy as jnp
from jax import lax
from jax.sharding import PartitionSpec as P

HD = 128


def rotate(vector, position):
    half_dim = vector.shape[-1] // 2
    frequency = 1000000.0 ** (-(jnp.arange(half_dim, dtype=jnp.float32) * 2.0 / vector.shape[-1]))
    angles = position.astype(jnp.float32)[..., None] * frequency
    cosine = jnp.concatenate([jnp.cos(angles), jnp.cos(angles)], -1)[..., None, :]
    sine = jnp.concatenate([jnp.sin(angles), jnp.sin(angles)], -1)[..., None, :]
    turned = jnp.concatenate([-vector[..., half_dim:], vector[..., :half_dim]], -1)
    return vector * cosine + turned * sine


def body(
    tokens,
    norm_gain,
    w_query,
    w_key,
    w_value,
    w_out,
    cache_keys,
    cache_values,
    cache_len,
    group_len,
):
    seq_index = lax.axis_index("seq")
    requests, local_rows, width_part = tokens.shape
    gathered = lax.all_gather(tokens, "tensor", axis=2, tiled=True).astype(jnp.float32)
    inverse_rms = lax.rsqrt(jnp.mean(gathered * gathered, -1, keepdims=True) + 1e-05)
    normed = (gathered * inverse_rms * norm_gain.astype(jnp.float32)).astype(jnp.bfloat16)
    flat_rows = normed.reshape(requests * local_rows, -1)
    heads_width = w_query.shape[1]
    local_heads = heads_width // HD

    def project(weight):
        return jnp.dot(flat_rows, weight, preferred_element_type=jnp.float32).reshape(
            requests, local_rows, local_heads, HD
        )

    offsets = jnp.arange(local_rows, dtype=jnp.int32)
    first_row = seq_index * local_rows
    position = cache_len[:, None] + first_row + offsets[None, :]
    queries = (
        rotate(project(w_query), position)
        .astype(jnp.bfloat16)
        .reshape(requests, local_rows, heads_width)
    )
    key_new = (
        rotate(project(w_key), position)
        .astype(jnp.bfloat16)
        .reshape(requests, local_rows, heads_width)
    )
    value_new = project(w_value).astype(jnp.bfloat16).reshape(requests, local_rows, heads_width)
    live_rows = (first_row + offsets)[None, :] < group_len[:, None]
    new_keys = jnp.where(live_rows[..., None], key_new, jnp.zeros_like(key_new))
    new_values = jnp.where(live_rows[..., None], value_new, jnp.zeros_like(value_new))
    seq_count = lax.axis_size("seq")
    group_total = seq_count * local_rows
    cache_slots = cache_keys.shape[1]
    head = seq_index % local_heads
    partner = seq_index + 1 - 2 * head
    swap = [(index, index + 1 - 2 * (index % 2)) for index in range(seq_count)]

    def own_head(array):
        return lax.dynamic_slice_in_dim(array, head * HD, HD, axis=2)

    def other_head(array):
        return lax.dynamic_slice_in_dim(array, (1 - head) * HD, HD, axis=2)

    cache_pair = lax.ppermute(
        jnp.concatenate([other_head(cache_keys), other_head(cache_values)], 1), "seq", swap
    )
    fresh_pair = lax.ppermute(
        jnp.concatenate([other_head(key_new), other_head(value_new)], 1), "seq", swap
    )
    pair_keys = jnp.concatenate([own_head(cache_keys), cache_pair[:, :cache_slots]], 1)
    pair_values = jnp.concatenate([own_head(cache_values), cache_pair[:, cache_slots:]], 1)
    group_keys = jnp.concatenate([own_head(key_new), fresh_pair[:, :local_rows]], 1)
    group_values = jnp.concatenate([own_head(value_new), fresh_pair[:, local_rows:]], 1)
    slot_arange = jnp.arange(cache_slots, dtype=jnp.int32)
    slot_index = jnp.concatenate(
        [seq_index * cache_slots + slot_arange, partner * cache_slots + slot_arange]
    )
    token_index = jnp.concatenate(
        [seq_index * local_rows + offsets, partner * local_rows + offsets]
    )
    query_heads = jnp.stack(
        [queries[:, :, h * HD : (h + 1) * HD] for h in range(local_heads)]
    ).reshape(local_heads, requests * local_rows, HD)
    query_sent = jnp.tile(query_heads, (seq_count // local_heads, 1, 1))
    query_got = lax.all_to_all(query_sent, "seq", 0, 0, tiled=True)
    query_index = jnp.arange(group_total, dtype=jnp.int32)
    score_scale = HD ** (-0.5)
    payload_list = []
    for request in range(requests):
        query_rows = query_got[:, request * local_rows : (request + 1) * local_rows].reshape(
            group_total, HD
        )
        cache_ok = (slot_index < cache_len[request])[None, :]
        group_ok = (token_index[None, :] <= query_index[:, None]) & (
            token_index < group_len[request]
        )[None, :]
        cache_scores = jnp.where(
            cache_ok,
            jnp.dot(query_rows, pair_keys[request].T, preferred_element_type=jnp.float32)
            * score_scale,
            -1e30,
        )
        group_scores = jnp.where(
            group_ok,
            jnp.dot(query_rows, group_keys[request].T, preferred_element_type=jnp.float32)
            * score_scale,
            -1e30,
        )
        row_peak = jnp.maximum(jnp.max(cache_scores, -1), jnp.max(group_scores, -1))
        cache_weights = jnp.where(cache_ok, jnp.exp(cache_scores - row_peak[:, None]), 0.0)
        group_weights = jnp.where(group_ok, jnp.exp(group_scores - row_peak[:, None]), 0.0)
        row_mass = jnp.sum(cache_weights, -1) + jnp.sum(group_weights, -1)
        numerators = jnp.dot(
            cache_weights.astype(jnp.bfloat16),
            pair_values[request],
            preferred_element_type=jnp.float32,
        ) + jnp.dot(
            group_weights.astype(jnp.bfloat16),
            group_values[request],
            preferred_element_type=jnp.float32,
        )
        stats = jnp.stack([row_peak, row_mass], -1).reshape(seq_count, 1, local_rows * 2)
        stats = jnp.pad(stats, ((0, 0), (0, 0), (0, HD - local_rows * 2)))
        payload_list.append(
            jnp.concatenate([numerators.reshape(seq_count, local_rows, HD), stats], 1)
        )
    block_rows = local_rows + 1
    attended_list = []
    for first in range(0, requests, 2):
        sent = jnp.concatenate(payload_list[first : first + 2], 1)
        arrived = lax.all_to_all(sent, "seq", 0, 0, tiled=True)
        for member in range(sent.shape[1] // block_rows):
            head_parts = []
            for h in range(local_heads):
                received = arrived[h::local_heads, member * block_rows : (member + 1) * block_rows]
                block_stats = received[:, local_rows, : local_rows * 2].reshape(-1, local_rows, 2)
                block_peak = block_stats[..., 0]
                factor = jnp.exp(block_peak - jnp.max(block_peak, 0))
                mass_sum = jnp.sum(block_stats[..., 1] * factor, 0)
                numer_sum = jnp.sum(received[:, :local_rows] * factor[..., None], 0)
                head_parts.append(numer_sum / mass_sum[:, None])
            attended_list.append(jnp.concatenate(head_parts, -1))
    attended = (
        jnp.where(live_rows[..., None], jnp.stack(attended_list), 0.0)
        .astype(jnp.bfloat16)
        .reshape(requests * local_rows, heads_width)
    )
    partial_out = jnp.dot(attended, w_out, preferred_element_type=jnp.float32).reshape(
        requests, local_rows, -1
    )
    mixed = lax.psum_scatter(partial_out, "tensor", scatter_dimension=2, tiled=True).astype(
        jnp.bfloat16
    )
    return (mixed, new_keys, new_values)


def solution(mesh):
    placed = (
        P(None, "seq", "tensor"),
        P(),
        P(None, "tensor"),
        P(None, "tensor"),
        P(None, "tensor"),
        P("tensor", None),
        P(None, "seq", "tensor"),
        P(None, "seq", "tensor"),
        P(),
        P(),
    )
    return jax.shard_map(
        body,
        mesh=mesh,
        in_specs=placed,
        out_specs=(P(None, "seq", "tensor"), P(None, "seq", "tensor"), P(None, "seq", "tensor")),
        check_vma=False,
    )
```

```python
import jax
import jax.numpy as jnp
from jax import lax
from jax.sharding import PartitionSpec as P

HD = 128


def rotate(vector, position):
    half_dim = vector.shape[-1] // 2
    frequency = 1000000.0 ** (-(jnp.arange(half_dim, dtype=jnp.float32) * 2.0 / vector.shape[-1]))
    angles = position.astype(jnp.float32)[..., None] * frequency
    cosine = jnp.concatenate([jnp.cos(angles), jnp.cos(angles)], -1)[..., None, :]
    sine = jnp.concatenate([jnp.sin(angles), jnp.sin(angles)], -1)[..., None, :]
    turned = jnp.concatenate([-vector[..., half_dim:], vector[..., :half_dim]], -1)
    return vector * cosine + turned * sine


def body(
    tokens,
    norm_gain,
    w_query,
    w_key,
    w_value,
    w_out,
    cache_keys,
    cache_values,
    cache_len,
    group_len,
):
    seq_index = lax.axis_index("seq")
    requests, local_rows, width_part = tokens.shape
    gathered = lax.all_gather(tokens, "tensor", axis=2, tiled=True).astype(jnp.float32)
    inverse_rms = lax.rsqrt(jnp.mean(gathered * gathered, -1, keepdims=True) + 1e-05)
    normed = (gathered * inverse_rms * norm_gain.astype(jnp.float32)).astype(jnp.bfloat16)
    flat_rows = normed.reshape(requests * local_rows, -1)
    heads_width = w_query.shape[1]
    local_heads = heads_width // HD

    def project(weight):
        return jnp.dot(flat_rows, weight, preferred_element_type=jnp.float32).reshape(
            requests, local_rows, local_heads, HD
        )

    offsets = jnp.arange(local_rows, dtype=jnp.int32)
    first_row = seq_index * local_rows
    position = cache_len[:, None] + first_row + offsets[None, :]
    queries = (
        rotate(project(w_query), position)
        .astype(jnp.bfloat16)
        .reshape(requests, local_rows, heads_width)
    )
    key_new = (
        rotate(project(w_key), position)
        .astype(jnp.bfloat16)
        .reshape(requests, local_rows, heads_width)
    )
    value_new = project(w_value).astype(jnp.bfloat16).reshape(requests, local_rows, heads_width)
    live_rows = (first_row + offsets)[None, :] < group_len[:, None]
    new_keys = jnp.where(live_rows[..., None], key_new, jnp.zeros_like(key_new))
    new_values = jnp.where(live_rows[..., None], value_new, jnp.zeros_like(value_new))
    seq_count = lax.axis_size("seq")
    group_total = seq_count * local_rows
    cache_slots = cache_keys.shape[1]
    head = seq_index % local_heads
    partner = seq_index + 1 - 2 * head
    swap = [(index, index + 1 - 2 * (index % 2)) for index in range(seq_count)]

    def own_head(array):
        return lax.dynamic_slice_in_dim(array, head * HD, HD, axis=2)

    def other_head(array):
        return lax.dynamic_slice_in_dim(array, (1 - head) * HD, HD, axis=2)

    cache_pair = lax.ppermute(
        jnp.concatenate([other_head(cache_keys), other_head(cache_values)], 1), "seq", swap
    )
    fresh_pair = lax.ppermute(
        jnp.concatenate([other_head(key_new), other_head(value_new)], 1), "seq", swap
    )
    pair_keys = jnp.concatenate([own_head(cache_keys), cache_pair[:, :cache_slots]], 1)
    pair_values = jnp.concatenate([own_head(cache_values), cache_pair[:, cache_slots:]], 1)
    group_keys = jnp.concatenate([own_head(key_new), fresh_pair[:, :local_rows]], 1)
    group_values = jnp.concatenate([own_head(value_new), fresh_pair[:, local_rows:]], 1)
    slot_arange = jnp.arange(cache_slots, dtype=jnp.int32)
    slot_index = jnp.concatenate(
        [seq_index * cache_slots + slot_arange, partner * cache_slots + slot_arange]
    )
    token_index = jnp.concatenate(
        [seq_index * local_rows + offsets, partner * local_rows + offsets]
    )
    query_heads = jnp.stack(
        [queries[:, :, h * HD : (h + 1) * HD] for h in range(local_heads)]
    ).reshape(local_heads, requests * local_rows, HD)
    query_sent = jnp.tile(query_heads, (seq_count // local_heads, 1, 1))
    query_got = lax.all_to_all(query_sent, "seq", 0, 0, tiled=True)
    query_index = jnp.arange(group_total, dtype=jnp.int32)
    score_scale = HD ** (-0.5)
    payload_list = []
    for request in range(requests):
        query_rows = query_got[:, request * local_rows : (request + 1) * local_rows].reshape(
            group_total, HD
        )
        cache_ok = (slot_index < cache_len[request])[None, :]
        group_ok = (token_index[None, :] <= query_index[:, None]) & (
            token_index < group_len[request]
        )[None, :]
        cache_scores = jnp.where(
            cache_ok,
            jnp.dot(query_rows, pair_keys[request].T, preferred_element_type=jnp.float32)
            * score_scale,
            -1e30,
        )
        group_scores = jnp.where(
            group_ok,
            jnp.dot(query_rows, group_keys[request].T, preferred_element_type=jnp.float32)
            * score_scale,
            -1e30,
        )
        row_peak = jnp.maximum(jnp.max(cache_scores, -1), jnp.max(group_scores, -1))
        cache_weights = jnp.where(cache_ok, jnp.exp(cache_scores - row_peak[:, None]), 0.0)
        group_weights = jnp.where(group_ok, jnp.exp(group_scores - row_peak[:, None]), 0.0)
        row_mass = jnp.sum(cache_weights, -1) + jnp.sum(group_weights, -1)
        numerators = jnp.dot(
            cache_weights.astype(jnp.bfloat16),
            pair_values[request],
            preferred_element_type=jnp.float32,
        ) + jnp.dot(
            group_weights.astype(jnp.bfloat16),
            group_values[request],
            preferred_element_type=jnp.float32,
        )
        stats = jnp.stack([row_peak, row_mass], -1).reshape(seq_count, 1, local_rows * 2)
        stats = jnp.pad(stats, ((0, 0), (0, 0), (0, HD - local_rows * 2)))
        payload_list.append(
            jnp.concatenate([numerators.reshape(seq_count, local_rows, HD), stats], 1)
        )
    block_rows = local_rows + 1
    attended_list = []
    mixed_list = []
    tensor_count = lax.axis_size("tensor")
    for first in range(0, requests, 2):
        sent = jnp.concatenate(payload_list[first : first + 2], 1)
        arrived = lax.all_to_all(sent, "seq", 0, 0, tiled=True)
        for member in range(sent.shape[1] // block_rows):
            head_parts = []
            for h in range(local_heads):
                received = arrived[h::local_heads, member * block_rows : (member + 1) * block_rows]
                block_stats = received[:, local_rows, : local_rows * 2].reshape(-1, local_rows, 2)
                block_peak = block_stats[..., 0]
                factor = jnp.exp(block_peak - jnp.max(block_peak, 0))
                mass_sum = jnp.sum(block_stats[..., 1] * factor, 0)
                numer_sum = jnp.sum(received[:, :local_rows] * factor[..., None], 0)
                head_parts.append(numer_sum / mass_sum[:, None])
            attended_list.append(jnp.concatenate(head_parts, -1))
        attended = (
            jnp.where(
                live_rows[first : first + 2, :, None],
                jnp.stack(attended_list[first : first + 2]),
                0.0,
            )
            .astype(jnp.bfloat16)
            .reshape(-1, heads_width)
        )
        partial_out = jnp.einsum(
            "rk,kcn->crn",
            attended,
            w_out.reshape(heads_width, tensor_count, -1),
            preferred_element_type=jnp.float32,
        )
        partial_sums = lax.all_to_all(partial_out, "tensor", 0, 0, tiled=True)
        mixed_list.append(
            jnp.sum(partial_sums, 0).astype(jnp.bfloat16).reshape(-1, local_rows, partial_out.shape[2])
        )
    mixed = jnp.concatenate(mixed_list, 0)
    return (mixed, new_keys, new_values)


def solution(mesh):
    placed = (
        P(None, "seq", "tensor"),
        P(),
        P(None, "tensor"),
        P(None, "tensor"),
        P(None, "tensor"),
        P("tensor", None),
        P(None, "seq", "tensor"),
        P(None, "seq", "tensor"),
        P(),
        P(),
    )
    return jax.shard_map(
        body,
        mesh=mesh,
        in_specs=placed,
        out_specs=(P(None, "seq", "tensor"), P(None, "seq", "tensor"), P(None, "seq", "tensor")),
        check_vma=False,
    )
```

```python
import jax
import jax.numpy as jnp
from jax import lax
from jax.sharding import PartitionSpec as P

HD = 128


def rotate(vector, position):
    half_dim = vector.shape[-1] // 2
    frequency = 1000000.0 ** (-(jnp.arange(half_dim, dtype=jnp.float32) * 2.0 / vector.shape[-1]))
    angles = position.astype(jnp.float32)[..., None] * frequency
    cosine = jnp.concatenate([jnp.cos(angles), jnp.cos(angles)], -1)[..., None, :]
    sine = jnp.concatenate([jnp.sin(angles), jnp.sin(angles)], -1)[..., None, :]
    turned = jnp.concatenate([-vector[..., half_dim:], vector[..., :half_dim]], -1)
    return vector * cosine + turned * sine


def body(
    tokens,
    norm_gain,
    w_query,
    w_key,
    w_value,
    w_out,
    cache_keys,
    cache_values,
    cache_len,
    group_len,
):
    seq_index = lax.axis_index("seq")
    requests, local_rows, width_part = tokens.shape
    token_copies = jnp.broadcast_to(tokens[None], (lax.axis_size("tensor"),) + tokens.shape)
    gathered = (
        lax.all_to_all(token_copies, "tensor", 0, 0, tiled=True)
        .transpose(1, 2, 0, 3)
        .reshape(requests, local_rows, -1)
        .astype(jnp.float32)
    )
    inverse_rms = lax.rsqrt(jnp.mean(gathered * gathered, -1, keepdims=True) + 1e-05)
    normed = (gathered * inverse_rms * norm_gain.astype(jnp.float32)).astype(jnp.bfloat16)
    flat_rows = normed.reshape(requests * local_rows, -1)
    heads_width = w_query.shape[1]
    local_heads = heads_width // HD

    def project(weight):
        return jnp.dot(flat_rows, weight, preferred_element_type=jnp.float32).reshape(
            requests, local_rows, local_heads, HD
        )

    offsets = jnp.arange(local_rows, dtype=jnp.int32)
    first_row = seq_index * local_rows
    position = cache_len[:, None] + first_row + offsets[None, :]
    queries = (
        rotate(project(w_query), position)
        .astype(jnp.bfloat16)
        .reshape(requests, local_rows, heads_width)
    )
    key_new = (
        rotate(project(w_key), position)
        .astype(jnp.bfloat16)
        .reshape(requests, local_rows, heads_width)
    )
    value_new = project(w_value).astype(jnp.bfloat16).reshape(requests, local_rows, heads_width)
    live_rows = (first_row + offsets)[None, :] < group_len[:, None]
    new_keys = jnp.where(live_rows[..., None], key_new, jnp.zeros_like(key_new))
    new_values = jnp.where(live_rows[..., None], value_new, jnp.zeros_like(value_new))
    seq_count = lax.axis_size("seq")
    group_total = seq_count * local_rows
    cache_slots = cache_keys.shape[1]
    head = seq_index % local_heads
    partner = seq_index + 1 - 2 * head
    swap = [(index, index + 1 - 2 * (index % 2)) for index in range(seq_count)]

    def own_head(array):
        return lax.dynamic_slice_in_dim(array, head * HD, HD, axis=2)

    def other_head(array):
        return lax.dynamic_slice_in_dim(array, (1 - head) * HD, HD, axis=2)

    cache_pair = lax.ppermute(
        jnp.concatenate([other_head(cache_keys), other_head(cache_values)], 1), "seq", swap
    )
    fresh_pair = lax.ppermute(
        jnp.concatenate([other_head(key_new), other_head(value_new)], 1), "seq", swap
    )
    pair_keys = jnp.concatenate([own_head(cache_keys), cache_pair[:, :cache_slots]], 1)
    pair_values = jnp.concatenate([own_head(cache_values), cache_pair[:, cache_slots:]], 1)
    group_keys = jnp.concatenate([own_head(key_new), fresh_pair[:, :local_rows]], 1)
    group_values = jnp.concatenate([own_head(value_new), fresh_pair[:, local_rows:]], 1)
    slot_arange = jnp.arange(cache_slots, dtype=jnp.int32)
    slot_index = jnp.concatenate(
        [seq_index * cache_slots + slot_arange, partner * cache_slots + slot_arange]
    )
    token_index = jnp.concatenate(
        [seq_index * local_rows + offsets, partner * local_rows + offsets]
    )
    query_heads = jnp.stack(
        [queries[:, :, h * HD : (h + 1) * HD] for h in range(local_heads)]
    ).reshape(local_heads, requests * local_rows, HD)
    query_sent = jnp.tile(query_heads, (seq_count // local_heads, 1, 1))
    query_got = lax.all_to_all(query_sent, "seq", 0, 0, tiled=True)
    query_index = jnp.arange(group_total, dtype=jnp.int32)
    score_scale = HD ** (-0.5)
    payload_list = []
    for request in range(requests):
        query_rows = query_got[:, request * local_rows : (request + 1) * local_rows].reshape(
            group_total, HD
        )
        cache_ok = (slot_index < cache_len[request])[None, :]
        group_ok = (token_index[None, :] <= query_index[:, None]) & (
            token_index < group_len[request]
        )[None, :]
        cache_scores = jnp.where(
            cache_ok,
            jnp.dot(query_rows, pair_keys[request].T, preferred_element_type=jnp.float32)
            * score_scale,
            -1e30,
        )
        group_scores = jnp.where(
            group_ok,
            jnp.dot(query_rows, group_keys[request].T, preferred_element_type=jnp.float32)
            * score_scale,
            -1e30,
        )
        row_peak = jnp.maximum(jnp.max(cache_scores, -1), jnp.max(group_scores, -1))
        cache_weights = jnp.where(cache_ok, jnp.exp(cache_scores - row_peak[:, None]), 0.0)
        group_weights = jnp.where(group_ok, jnp.exp(group_scores - row_peak[:, None]), 0.0)
        row_mass = jnp.sum(cache_weights, -1) + jnp.sum(group_weights, -1)
        numerators = jnp.dot(
            cache_weights.astype(jnp.bfloat16),
            pair_values[request],
            preferred_element_type=jnp.float32,
        ) + jnp.dot(
            group_weights.astype(jnp.bfloat16),
            group_values[request],
            preferred_element_type=jnp.float32,
        )
        stats = jnp.stack([row_peak, row_mass], -1).reshape(seq_count, 1, local_rows * 2)
        stats = jnp.pad(stats, ((0, 0), (0, 0), (0, HD - local_rows * 2)))
        payload_list.append(
            jnp.concatenate([numerators.reshape(seq_count, local_rows, HD), stats], 1)
        )
    block_rows = local_rows + 1
    attended_list = []
    mixed_list = []
    tensor_count = lax.axis_size("tensor")
    for first in range(0, requests, 2):
        sent = jnp.concatenate(payload_list[first : first + 2], 1)
        arrived = lax.all_to_all(sent, "seq", 0, 0, tiled=True)
        for member in range(sent.shape[1] // block_rows):
            head_parts = []
            for h in range(local_heads):
                received = arrived[h::local_heads, member * block_rows : (member + 1) * block_rows]
                block_stats = received[:, local_rows, : local_rows * 2].reshape(-1, local_rows, 2)
                block_peak = block_stats[..., 0]
                factor = jnp.exp(block_peak - jnp.max(block_peak, 0))
                mass_sum = jnp.sum(block_stats[..., 1] * factor, 0)
                numer_sum = jnp.sum(received[:, :local_rows] * factor[..., None], 0)
                head_parts.append(numer_sum / mass_sum[:, None])
            attended_list.append(jnp.concatenate(head_parts, -1))
        attended = (
            jnp.where(
                live_rows[first : first + 2, :, None],
                jnp.stack(attended_list[first : first + 2]),
                0.0,
            )
            .astype(jnp.bfloat16)
            .reshape(-1, heads_width)
        )
        partial_out = jnp.einsum(
            "rk,kcn->crn",
            attended,
            w_out.reshape(heads_width, tensor_count, -1),
            preferred_element_type=jnp.float32,
        )
        partial_sums = lax.all_to_all(partial_out, "tensor", 0, 0, tiled=True)
        mixed_list.append(
            jnp.sum(partial_sums, 0).astype(jnp.bfloat16).reshape(-1, local_rows, partial_out.shape[2])
        )
    mixed = jnp.concatenate(mixed_list, 0)
    return (mixed, new_keys, new_values)


def solution(mesh):
    placed = (
        P(None, "seq", "tensor"),
        P(),
        P(None, "tensor"),
        P(None, "tensor"),
        P(None, "tensor"),
        P("tensor", None),
        P(None, "seq", "tensor"),
        P(None, "seq", "tensor"),
        P(),
        P(),
    )
    return jax.shard_map(
        body,
        mesh=mesh,
        in_specs=placed,
        out_specs=(P(None, "seq", "tensor"), P(None, "seq", "tensor"), P(None, "seq", "tensor")),
        check_vma=False,
    )
```

```python
import jax
import jax.numpy as jnp
from jax import lax
from jax.sharding import PartitionSpec as P

HD = 128


def rotate(vector, position):
    half_dim = vector.shape[-1] // 2
    frequency = 1000000.0 ** (-(jnp.arange(half_dim, dtype=jnp.float32) * 2.0 / vector.shape[-1]))
    angles = position.astype(jnp.float32)[..., None] * frequency
    cosine = jnp.concatenate([jnp.cos(angles), jnp.cos(angles)], -1)[..., None, :]
    sine = jnp.concatenate([jnp.sin(angles), jnp.sin(angles)], -1)[..., None, :]
    turned = jnp.concatenate([-vector[..., half_dim:], vector[..., :half_dim]], -1)
    return vector * cosine + turned * sine


def body(
    tokens,
    norm_gain,
    w_query,
    w_key,
    w_value,
    w_out,
    cache_keys,
    cache_values,
    cache_len,
    group_len,
):
    seq_index = lax.axis_index("seq")
    requests, local_rows, width_part = tokens.shape
    token_copies = jnp.broadcast_to(tokens[None], (lax.axis_size("tensor"),) + tokens.shape)
    gathered = (
        lax.all_to_all(token_copies, "tensor", 0, 0, tiled=True)
        .transpose(1, 2, 0, 3)
        .reshape(requests, local_rows, -1)
        .astype(jnp.float32)
    )
    inverse_rms = lax.rsqrt(jnp.mean(gathered * gathered, -1, keepdims=True) + 1e-05)
    normed = (gathered * inverse_rms * norm_gain.astype(jnp.float32)).astype(jnp.bfloat16)
    flat_rows = normed.reshape(requests * local_rows, -1)
    heads_width = w_query.shape[1]
    local_heads = heads_width // HD

    def project(weight):
        return jnp.dot(flat_rows, weight, preferred_element_type=jnp.float32).reshape(
            requests, local_rows, local_heads, HD
        )

    offsets = jnp.arange(local_rows, dtype=jnp.int32)
    first_row = seq_index * local_rows
    position = cache_len[:, None] + first_row + offsets[None, :]
    queries = (
        rotate(project(w_query), position)
        .astype(jnp.bfloat16)
        .reshape(requests, local_rows, heads_width)
    )
    key_new = (
        rotate(project(w_key), position)
        .astype(jnp.bfloat16)
        .reshape(requests, local_rows, heads_width)
    )
    value_new = project(w_value).astype(jnp.bfloat16).reshape(requests, local_rows, heads_width)
    live_rows = (first_row + offsets)[None, :] < group_len[:, None]
    new_keys = jnp.where(live_rows[..., None], key_new, jnp.zeros_like(key_new))
    new_values = jnp.where(live_rows[..., None], value_new, jnp.zeros_like(value_new))
    seq_count = lax.axis_size("seq")
    group_total = seq_count * local_rows
    cache_slots = cache_keys.shape[1]
    head = seq_index % local_heads
    partner = seq_index + 1 - 2 * head
    swap = [(index, index + 1 - 2 * (index % 2)) for index in range(seq_count)]

    def own_head(array):
        return lax.dynamic_slice_in_dim(array, head * HD, HD, axis=2)

    def other_head(array):
        return lax.dynamic_slice_in_dim(array, (1 - head) * HD, HD, axis=2)

    cache_pair = lax.ppermute(
        jnp.concatenate([other_head(cache_keys), other_head(cache_values)], 1), "seq", swap
    )
    fresh_pair = lax.ppermute(
        jnp.concatenate([other_head(key_new), other_head(value_new)], 1), "seq", swap
    )
    pair_keys = jnp.concatenate([own_head(cache_keys), cache_pair[:, :cache_slots]], 1)
    pair_values = jnp.concatenate([own_head(cache_values), cache_pair[:, cache_slots:]], 1)
    group_keys = jnp.concatenate([own_head(key_new), fresh_pair[:, :local_rows]], 1)
    group_values = jnp.concatenate([own_head(value_new), fresh_pair[:, local_rows:]], 1)
    slot_arange = jnp.arange(cache_slots, dtype=jnp.int32)
    slot_index = jnp.concatenate(
        [seq_index * cache_slots + slot_arange, partner * cache_slots + slot_arange]
    )
    token_index = jnp.concatenate(
        [seq_index * local_rows + offsets, partner * local_rows + offsets]
    )
    query_heads = jnp.stack(
        [queries[:, :, h * HD : (h + 1) * HD] for h in range(local_heads)]
    ).reshape(local_heads, requests * local_rows, HD)
    query_sent = jnp.tile(query_heads, (seq_count // local_heads, 1, 1))
    query_got = lax.all_to_all(query_sent, "seq", 0, 0, tiled=True)
    query_index = jnp.arange(group_total, dtype=jnp.int32)
    score_scale = HD ** (-0.5)
    payload_list = []
    for request in range(requests):
        query_rows = query_got[:, request * local_rows : (request + 1) * local_rows].reshape(
            group_total, HD
        )
        cache_ok = (slot_index < cache_len[request])[None, :]
        group_ok = (token_index[None, :] <= query_index[:, None]) & (
            token_index < group_len[request]
        )[None, :]
        cache_scores = jnp.where(
            cache_ok,
            jnp.dot(query_rows, pair_keys[request].T, preferred_element_type=jnp.float32)
            * score_scale,
            -1e30,
        )
        group_scores = jnp.where(
            group_ok,
            jnp.dot(query_rows, group_keys[request].T, preferred_element_type=jnp.float32)
            * score_scale,
            -1e30,
        )
        row_peak = jnp.maximum(jnp.max(cache_scores, -1), jnp.max(group_scores, -1))
        cache_weights = jnp.where(cache_ok, jnp.exp(cache_scores - row_peak[:, None]), 0.0)
        group_weights = jnp.where(group_ok, jnp.exp(group_scores - row_peak[:, None]), 0.0)
        row_mass = jnp.sum(cache_weights, -1) + jnp.sum(group_weights, -1)
        numerators = jnp.dot(
            cache_weights.astype(jnp.bfloat16),
            pair_values[request],
            preferred_element_type=jnp.float32,
        ) + jnp.dot(
            group_weights.astype(jnp.bfloat16),
            group_values[request],
            preferred_element_type=jnp.float32,
        )
        stats = jnp.stack([row_peak, row_mass], -1).reshape(seq_count, 1, local_rows * 2)
        stats = jnp.pad(stats, ((0, 0), (0, 0), (0, HD - local_rows * 2)))
        payload_list.append(
            jnp.concatenate([numerators.reshape(seq_count, local_rows, HD), stats], 1)
        )
    block_rows = local_rows + 1
    attended_list = []
    tensor_count = lax.axis_size("tensor")
    for first in range(0, requests, 2):
        sent = jnp.concatenate(payload_list[first : first + 2], 1)
        arrived = lax.all_to_all(sent, "seq", 0, 0, tiled=True)
        for member in range(sent.shape[1] // block_rows):
            head_parts = []
            for h in range(local_heads):
                received = arrived[h::local_heads, member * block_rows : (member + 1) * block_rows]
                block_stats = received[:, local_rows, : local_rows * 2].reshape(-1, local_rows, 2)
                block_peak = block_stats[..., 0]
                factor = jnp.exp(block_peak - jnp.max(block_peak, 0))
                mass_sum = jnp.sum(block_stats[..., 1] * factor, 0)
                numer_sum = jnp.sum(received[:, :local_rows] * factor[..., None], 0)
                head_parts.append(numer_sum / mass_sum[:, None])
            attended_list.append(jnp.concatenate(head_parts, -1))
    attended = (
        jnp.where(live_rows[..., None], jnp.stack(attended_list), 0.0)
        .astype(jnp.bfloat16)
        .reshape(requests * local_rows, heads_width)
    )
    partial_out = jnp.einsum(
        "rk,kcn->crn",
        attended,
        w_out.reshape(heads_width, tensor_count, -1),
        preferred_element_type=jnp.float32,
    )
    partial_sums = lax.all_to_all(partial_out, "tensor", 0, 0, tiled=True)
    mixed = (
        jnp.sum(partial_sums, 0)
        .astype(jnp.bfloat16)
        .reshape(requests, local_rows, partial_out.shape[2])
    )
    return (mixed, new_keys, new_values)


def solution(mesh):
    placed = (
        P(None, "seq", "tensor"),
        P(),
        P(None, "tensor"),
        P(None, "tensor"),
        P(None, "tensor"),
        P("tensor", None),
        P(None, "seq", "tensor"),
        P(None, "seq", "tensor"),
        P(),
        P(),
    )
    return jax.shard_map(
        body,
        mesh=mesh,
        in_specs=placed,
        out_specs=(P(None, "seq", "tensor"), P(None, "seq", "tensor"), P(None, "seq", "tensor")),
        check_vma=False,
    )
```

```python
import jax
import jax.numpy as jnp
from jax import lax
from jax.sharding import PartitionSpec as P

HD = 128


def rotate(vector, position):
    half_dim = vector.shape[-1] // 2
    frequency = 1000000.0 ** (-(jnp.arange(half_dim, dtype=jnp.float32) * 2.0 / vector.shape[-1]))
    angles = position.astype(jnp.float32)[..., None] * frequency
    cosine = jnp.concatenate([jnp.cos(angles), jnp.cos(angles)], -1)[..., None, :]
    sine = jnp.concatenate([jnp.sin(angles), jnp.sin(angles)], -1)[..., None, :]
    turned = jnp.concatenate([-vector[..., half_dim:], vector[..., :half_dim]], -1)
    return vector * cosine + turned * sine


def body(
    tokens,
    norm_gain,
    w_query,
    w_key,
    w_value,
    w_out,
    cache_keys,
    cache_values,
    cache_len,
    group_len,
):
    seq_index = lax.axis_index("seq")
    requests, local_rows, width_part = tokens.shape
    token_copies = jnp.broadcast_to(tokens[None], (lax.axis_size("tensor"),) + tokens.shape)
    gathered = (
        lax.all_to_all(token_copies, "tensor", 0, 0, tiled=True)
        .transpose(1, 2, 0, 3)
        .reshape(requests, local_rows, -1)
        .astype(jnp.float32)
    )
    inverse_rms = lax.rsqrt(jnp.mean(gathered * gathered, -1, keepdims=True) + 1e-05)
    normed = (gathered * inverse_rms * norm_gain.astype(jnp.float32)).astype(jnp.bfloat16)
    flat_rows = normed.reshape(requests * local_rows, -1)
    heads_width = w_query.shape[1]
    local_heads = heads_width // HD

    def project(weight):
        return jnp.dot(flat_rows, weight, preferred_element_type=jnp.float32).reshape(
            requests, local_rows, local_heads, HD
        )

    offsets = jnp.arange(local_rows, dtype=jnp.int32)
    first_row = seq_index * local_rows
    position = cache_len[:, None] + first_row + offsets[None, :]
    queries = (
        rotate(project(w_query), position)
        .astype(jnp.bfloat16)
        .reshape(requests, local_rows, heads_width)
    )
    key_new = (
        rotate(project(w_key), position)
        .astype(jnp.bfloat16)
        .reshape(requests, local_rows, heads_width)
    )
    value_new = project(w_value).astype(jnp.bfloat16).reshape(requests, local_rows, heads_width)
    live_rows = (first_row + offsets)[None, :] < group_len[:, None]
    new_keys = jnp.where(live_rows[..., None], key_new, jnp.zeros_like(key_new))
    new_values = jnp.where(live_rows[..., None], value_new, jnp.zeros_like(value_new))
    seq_count = lax.axis_size("seq")
    group_total = seq_count * local_rows
    cache_slots = cache_keys.shape[1]
    head = seq_index % local_heads
    partner = seq_index + 1 - 2 * head
    swap = [(index, index + 1 - 2 * (index % 2)) for index in range(seq_count)]

    def own_head(array):
        return lax.dynamic_slice_in_dim(array, head * HD, HD, axis=2)

    def other_head(array):
        return lax.dynamic_slice_in_dim(array, (1 - head) * HD, HD, axis=2)

    cache_pair = lax.ppermute(
        jnp.concatenate([other_head(cache_keys), other_head(cache_values)], 1), "seq", swap
    )
    fresh_pair = lax.ppermute(
        jnp.concatenate([other_head(key_new), other_head(value_new)], 1), "seq", swap
    )
    pair_keys = jnp.concatenate([own_head(cache_keys), cache_pair[:, :cache_slots]], 1)
    pair_values = jnp.concatenate([own_head(cache_values), cache_pair[:, cache_slots:]], 1)
    group_keys = jnp.concatenate([own_head(key_new), fresh_pair[:, :local_rows]], 1)
    group_values = jnp.concatenate([own_head(value_new), fresh_pair[:, local_rows:]], 1)
    slot_arange = jnp.arange(cache_slots, dtype=jnp.int32)
    slot_index = jnp.concatenate(
        [seq_index * cache_slots + slot_arange, partner * cache_slots + slot_arange]
    )
    token_index = jnp.concatenate(
        [seq_index * local_rows + offsets, partner * local_rows + offsets]
    )
    query_heads = jnp.stack(
        [queries[:, :, h * HD : (h + 1) * HD] for h in range(local_heads)]
    ).reshape(local_heads, requests * local_rows, HD)
    query_sent = jnp.tile(query_heads, (seq_count // local_heads, 1, 1))
    query_got = lax.all_to_all(query_sent, "seq", 0, 0, tiled=True)
    query_index = jnp.arange(group_total, dtype=jnp.int32)
    score_scale = HD ** (-0.5)
    payload_list = []
    for request in range(requests):
        query_rows = query_got[:, request * local_rows : (request + 1) * local_rows].reshape(
            group_total, HD
        )
        cache_ok = (slot_index < cache_len[request])[None, :]
        group_ok = (token_index[None, :] <= query_index[:, None]) & (
            token_index < group_len[request]
        )[None, :]
        cache_scores = jnp.where(
            cache_ok,
            jnp.dot(query_rows, pair_keys[request].T, preferred_element_type=jnp.float32)
            * score_scale,
            -1e30,
        )
        group_scores = jnp.where(
            group_ok,
            jnp.dot(query_rows, group_keys[request].T, preferred_element_type=jnp.float32)
            * score_scale,
            -1e30,
        )
        row_peak = jnp.maximum(jnp.max(cache_scores, -1), jnp.max(group_scores, -1))
        cache_weights = jnp.where(cache_ok, jnp.exp(cache_scores - row_peak[:, None]), 0.0)
        group_weights = jnp.where(group_ok, jnp.exp(group_scores - row_peak[:, None]), 0.0)
        row_mass = jnp.sum(cache_weights, -1) + jnp.sum(group_weights, -1)
        numerators = jnp.dot(
            cache_weights.astype(jnp.bfloat16),
            pair_values[request],
            preferred_element_type=jnp.float32,
        ) + jnp.dot(
            group_weights.astype(jnp.bfloat16),
            group_values[request],
            preferred_element_type=jnp.float32,
        )
        stats = jnp.stack([row_peak, row_mass], -1).reshape(seq_count, 1, local_rows * 2)
        stats = jnp.pad(stats, ((0, 0), (0, 0), (0, HD - local_rows * 2)))
        payload_list.append(
            jnp.concatenate([numerators.reshape(seq_count, local_rows, HD), stats], 1)
        )
    block_rows = local_rows + 1
    attended_list = []
    mixed_list = []
    tensor_count = lax.axis_size("tensor")
    for first in range(0, requests, 2):
        sent = jnp.concatenate(payload_list[first : first + 2], 1)
        arrived = lax.all_to_all(sent, "seq", 0, 0, tiled=True)
        members = sent.shape[1] // block_rows
        grouped = arrived.reshape(-1, local_heads, members, block_rows, HD)
        block_stats = grouped[:, :, :, local_rows, : local_rows * 2].reshape(
            -1, local_heads, members, local_rows, 2
        )
        block_peak = block_stats[..., 0]
        factor = jnp.exp(block_peak - jnp.max(block_peak, 0))
        mass_sum = jnp.sum(block_stats[..., 1] * factor, 0)
        numer_sum = jnp.sum(grouped[:, :, :, :local_rows] * factor[..., None], 0)
        pair_attended = (numer_sum / mass_sum[..., None]).transpose(1, 2, 0, 3)
        attended_list.extend(
            pair_attended.reshape(members, local_rows, heads_width)[member]
            for member in range(members)
        )
        attended = (
            jnp.where(
                live_rows[first : first + 2, :, None],
                jnp.stack(attended_list[first : first + 2]),
                0.0,
            )
            .astype(jnp.bfloat16)
            .reshape(-1, heads_width)
        )
        partial_out = jnp.einsum(
            "rk,kcn->crn",
            attended,
            w_out.reshape(heads_width, tensor_count, -1),
            preferred_element_type=jnp.float32,
        )
        partial_sums = lax.all_to_all(partial_out, "tensor", 0, 0, tiled=True)
        mixed_list.append(
            jnp.sum(partial_sums, 0).astype(jnp.bfloat16).reshape(-1, local_rows, partial_out.shape[2])
        )
    mixed = jnp.concatenate(mixed_list, 0)
    return (mixed, new_keys, new_values)


def solution(mesh):
    placed = (
        P(None, "seq", "tensor"),
        P(),
        P(None, "tensor"),
        P(None, "tensor"),
        P(None, "tensor"),
        P("tensor", None),
        P(None, "seq", "tensor"),
        P(None, "seq", "tensor"),
        P(),
        P(),
    )
    return jax.shard_map(
        body,
        mesh=mesh,
        in_specs=placed,
        out_specs=(P(None, "seq", "tensor"), P(None, "seq", "tensor"), P(None, "seq", "tensor")),
        check_vma=False,
    )
```

```python
import jax
import jax.numpy as jnp
from jax import lax
from jax.sharding import PartitionSpec as P

HD = 128


def rotate(vector, position):
    half_dim = vector.shape[-1] // 2
    frequency = 1000000.0 ** (-(jnp.arange(half_dim, dtype=jnp.float32) * 2.0 / vector.shape[-1]))
    angles = position.astype(jnp.float32)[..., None] * frequency
    cosine = jnp.concatenate([jnp.cos(angles), jnp.cos(angles)], -1)[..., None, :]
    sine = jnp.concatenate([jnp.sin(angles), jnp.sin(angles)], -1)[..., None, :]
    turned = jnp.concatenate([-vector[..., half_dim:], vector[..., :half_dim]], -1)
    return vector * cosine + turned * sine


def body(
    tokens,
    norm_gain,
    w_query,
    w_key,
    w_value,
    w_out,
    cache_keys,
    cache_values,
    cache_len,
    group_len,
):
    seq_index = lax.axis_index("seq")
    requests, local_rows, width_part = tokens.shape
    token_copies = jnp.broadcast_to(tokens[None], (lax.axis_size("tensor"),) + tokens.shape)
    gathered = (
        lax.all_to_all(token_copies, "tensor", 0, 0, tiled=True)
        .transpose(1, 2, 0, 3)
        .reshape(requests, local_rows, -1)
        .astype(jnp.float32)
    )
    inverse_rms = lax.rsqrt(jnp.mean(gathered * gathered, -1, keepdims=True) + 1e-05)
    normed = (gathered * inverse_rms * norm_gain.astype(jnp.float32)).astype(jnp.bfloat16)
    flat_rows = normed.reshape(requests * local_rows, -1)
    heads_width = w_query.shape[1]
    local_heads = heads_width // HD

    def project(weight):
        return jnp.dot(flat_rows, weight, preferred_element_type=jnp.float32).reshape(
            requests, local_rows, local_heads, HD
        )

    offsets = jnp.arange(local_rows, dtype=jnp.int32)
    first_row = seq_index * local_rows
    position = cache_len[:, None] + first_row + offsets[None, :]
    queries = (
        rotate(project(w_query), position)
        .astype(jnp.bfloat16)
        .reshape(requests, local_rows, heads_width)
    )
    key_new = (
        rotate(project(w_key), position)
        .astype(jnp.bfloat16)
        .reshape(requests, local_rows, heads_width)
    )
    value_new = project(w_value).astype(jnp.bfloat16).reshape(requests, local_rows, heads_width)
    live_rows = (first_row + offsets)[None, :] < group_len[:, None]
    new_keys = jnp.where(live_rows[..., None], key_new, jnp.zeros_like(key_new))
    new_values = jnp.where(live_rows[..., None], value_new, jnp.zeros_like(value_new))
    seq_count = lax.axis_size("seq")
    group_total = seq_count * local_rows
    cache_slots = cache_keys.shape[1]
    head = seq_index % local_heads
    partner = seq_index + 1 - 2 * head
    swap = [(index, index + 1 - 2 * (index % 2)) for index in range(seq_count)]

    def own_head(array):
        return lax.dynamic_slice_in_dim(array, head * HD, HD, axis=2)

    def other_head(array):
        return lax.dynamic_slice_in_dim(array, (1 - head) * HD, HD, axis=2)

    cache_pair = lax.ppermute(
        jnp.concatenate([other_head(cache_keys), other_head(cache_values)], 1), "seq", swap
    )
    fresh_pair = lax.ppermute(
        jnp.concatenate([other_head(key_new), other_head(value_new)], 1), "seq", swap
    )
    pair_keys = jnp.concatenate([own_head(cache_keys), cache_pair[:, :cache_slots]], 1)
    pair_values = jnp.concatenate([own_head(cache_values), cache_pair[:, cache_slots:]], 1)
    group_keys = jnp.concatenate([own_head(key_new), fresh_pair[:, :local_rows]], 1)
    group_values = jnp.concatenate([own_head(value_new), fresh_pair[:, local_rows:]], 1)
    slot_arange = jnp.arange(cache_slots, dtype=jnp.int32)
    slot_index = jnp.concatenate(
        [seq_index * cache_slots + slot_arange, partner * cache_slots + slot_arange]
    )
    token_index = jnp.concatenate(
        [seq_index * local_rows + offsets, partner * local_rows + offsets]
    )
    query_heads = jnp.stack(
        [queries[:, :, h * HD : (h + 1) * HD] for h in range(local_heads)]
    ).reshape(local_heads, requests * local_rows, HD)
    query_sent = jnp.tile(query_heads, (seq_count // local_heads, 1, 1))
    query_got = lax.all_to_all(query_sent, "seq", 0, 0, tiled=True)
    query_index = jnp.arange(group_total, dtype=jnp.int32)
    score_scale = HD ** (-0.5)
    payload_list = []
    for request in range(requests):
        query_rows = query_got[:, request * local_rows : (request + 1) * local_rows].reshape(
            group_total, HD
        )
        cache_ok = (slot_index < cache_len[request])[None, :]
        group_ok = (token_index[None, :] <= query_index[:, None]) & (
            token_index < group_len[request]
        )[None, :]
        cache_scores = jnp.where(
            cache_ok,
            jnp.dot(query_rows, pair_keys[request].T, preferred_element_type=jnp.float32)
            * score_scale,
            -1e30,
        )
        group_scores = jnp.where(
            group_ok,
            jnp.dot(query_rows, group_keys[request].T, preferred_element_type=jnp.float32)
            * score_scale,
            -1e30,
        )
        row_peak = jnp.maximum(jnp.max(cache_scores, -1), jnp.max(group_scores, -1))
        cache_weights = jnp.where(cache_ok, jnp.exp(cache_scores - row_peak[:, None]), 0.0)
        group_weights = jnp.where(group_ok, jnp.exp(group_scores - row_peak[:, None]), 0.0)
        row_mass = jnp.sum(cache_weights, -1) + jnp.sum(group_weights, -1)
        numerators = jnp.dot(
            cache_weights.astype(jnp.bfloat16),
            pair_values[request],
            preferred_element_type=jnp.float32,
        ) + jnp.dot(
            group_weights.astype(jnp.bfloat16),
            group_values[request],
            preferred_element_type=jnp.float32,
        )
        stats = jnp.stack([row_peak, row_mass], -1).reshape(seq_count, 1, local_rows * 2)
        stats = jnp.pad(stats, ((0, 0), (0, 0), (0, HD - local_rows * 2)))
        payload_list.append(
            jnp.concatenate([numerators.reshape(seq_count, local_rows, HD), stats], 1)
        )
    block_rows = local_rows + 1
    attended_list = []
    mixed_list = []
    tensor_count = lax.axis_size("tensor")
    for first in range(0, requests, 2):
        sent = jnp.concatenate(payload_list[first : first + 2], 1)
        arrived = lax.all_to_all(sent, "seq", 0, 0, tiled=True)
        members = sent.shape[1] // block_rows
        grouped = arrived.reshape(-1, local_heads, members, block_rows, HD)
        block_stats = grouped[:, :, :, local_rows, : local_rows * 2].reshape(
            -1, local_heads, members, local_rows, 2
        )
        block_peak = block_stats[..., 0]
        factor = jnp.exp(block_peak - jnp.max(block_peak, 0))
        mass_sum = jnp.sum(block_stats[..., 1] * factor, 0)
        numer_sum = jnp.sum(grouped[:, :, :, :local_rows] * factor[..., None], 0)
        pair_attended = (numer_sum / mass_sum[..., None]).transpose(1, 2, 0, 3)
        attended_list.extend(
            pair_attended.reshape(members, local_rows, heads_width)[member]
            for member in range(members)
        )
        attended = (
            jnp.where(
                live_rows[first : first + 2, :, None],
                jnp.stack(attended_list[first : first + 2]),
                0.0,
            )
            .astype(jnp.bfloat16)
            .reshape(-1, heads_width)
        )
        partial_out = jnp.einsum(
            "rk,kcn->crn",
            attended,
            w_out.reshape(heads_width, tensor_count, -1),
            preferred_element_type=jnp.float32,
        )
        partial_sums = lax.all_to_all(
            partial_out.astype(jnp.bfloat16), "tensor", 0, 0, tiled=True
        ).astype(jnp.float32)
        mixed_list.append(
            jnp.sum(partial_sums, 0).astype(jnp.bfloat16).reshape(-1, local_rows, partial_out.shape[2])
        )
    mixed = jnp.concatenate(mixed_list, 0)
    return (mixed, new_keys, new_values)


def solution(mesh):
    placed = (
        P(None, "seq", "tensor"),
        P(),
        P(None, "tensor"),
        P(None, "tensor"),
        P(None, "tensor"),
        P("tensor", None),
        P(None, "seq", "tensor"),
        P(None, "seq", "tensor"),
        P(),
        P(),
    )
    return jax.shard_map(
        body,
        mesh=mesh,
        in_specs=placed,
        out_specs=(P(None, "seq", "tensor"), P(None, "seq", "tensor"), P(None, "seq", "tensor")),
        check_vma=False,
    )
```
